32 devices in a mesh: groups: 2 (over x), energy: 8 (over z, y), space: 2 (over core).
Axes of the slice: x: 2, y: 2, z: 4, core: 2. Of those that a mesh axis runs over, the one named last changes fastest.
Arguments:
- ham_diag: float32 [2, 2, 512, 256], P('space', None, 'groups'), parts along dimension 2, as said below
- ham_coupling: float32 [2, 2, 256, 256], P('groups'), parts along dimension 0, may hold values from -0.25 to 0.25
- sigma_shift: float32 [8, 2, 512], P('energy', 'space', 'groups'), parts along dimension 2, may hold values from -3 to 3
- sigma_width: float32 [8, 2, 512], P('energy', 'space', 'groups'), parts along dimension 2, may hold values from 0.5 to 2
- occupation: float32 [8, 2, 512], P('energy', 'space', 'groups'), parts along dimension 2, may hold values from 0 to 1
Outputs:
- polarization: float32 [16, 2, 2, 256, 256], P('groups', None, None, ('energy', 'space')), parts along dimension 0
The draws below stay inside these ranges and needn't reach their ends.
There are 2 independent parts, one for each index of `groups`. The reference program is written for one: setup_inputs(seed, part) draws one part's arguments, and reference() takes and returns one part's arrays. A program takes and returns all parts, laid end to end along the dimension named above; each array names one. Nothing has to cross between parts.
Inputs may be any that keep to these rules, and one draw needn't show every extreme that they name: Each ham_diag[b, 0] is symmetric and each ham_diag[b, 1] antisymmetric.
All inputs are finite; a program needn't handle non-finite values.
Results may differ from the reference program's by a relative error of at most 0.0001.
Values sent between devices are 32-bit elements; how exact they have to be, the bound alone decides.
No kernel may reach another device: no remote copies, remote signals or barrier semaphores. Data moves between devices by JAX's collectives and lax.ppermute only.
A program may use at most 64 MiB of HBM per device.

```python
import math
import jax
import jax.numpy as jnp
from jax import lax

NORB = 256
NBLK = 2
NE = 8


def draw_ham_diag(key, part):
    first_key, second_key = jax.random.split(key)
    first = jax.random.truncated_normal(first_key, -3.0, 3.0, (NBLK, NORB, NORB), jnp.float32)
    second = jax.random.truncated_normal(second_key, -3.0, 3.0, (NBLK, NORB, NORB), jnp.float32)
    factor = 0.5 / NORB ** 0.5
    real_part = (first + jnp.swapaxes(first, 1, 2)) * factor
    imag_part = (second - jnp.swapaxes(second, 1, 2)) * factor
    return jnp.stack([real_part, imag_part], axis=1).astype(jnp.float32)


def levels(rng, dims, shards, low, largest):
    factor_of, own = 1.0, jax.random.fold_in(rng, 6)
    for dim, blocks in shards:
        steps = jnp.exp(jax.random.uniform(jax.random.fold_in(own, dim), (blocks,), jnp.float32, low / len(shards), largest / len(shards)))
        factor_of = factor_of * jnp.repeat(steps, dims[dim] // blocks).reshape([-1 if axis == dim else 1 for axis in range(len(dims))])
    return factor_of


def normal_values(stream_key, dims, width, reach, shards=(), kind=jnp.bfloat16):
    level = levels(stream_key, dims, shards, -0.22, 0.18) if shards else 1.0
    entries = jax.random.normal(stream_key, dims, jnp.float32) * width * level
    return jnp.minimum(jnp.maximum(entries, -reach), reach).astype(kind)


def setup_inputs(seed: int = 0, part: int = 0) -> dict:
    key_list = jax.random.split(jax.random.key(seed), 6)
    part_keys = jax.random.split(jax.random.fold_in(key_list[5], part), 6)
    ham_diag = draw_ham_diag(jax.random.fold_in(jax.random.fold_in(key_list[5], part), 71), part)
    ham_coupling = normal_values(part_keys[1], (NBLK - 1, 2, NORB, NORB), (2 * NORB) ** -0.5, 0.25, (), jnp.float32)
    sigma_shift = normal_values(part_keys[2], (NE, NBLK, NORB), 0.5, 3.0, ((0, 8), (1, 2)), jnp.float32)
    sigma_width = jnp.clip(jnp.exp(math.log(2.0) - 1.3862944 * jax.random.uniform(part_keys[3], (NE, NBLK, NORB), jnp.float32) ** levels(part_keys[3], (NE, NBLK, NORB), ((0, 8), (1, 2)), -0.2, 0.2)), 0.5, 2.0)
    occupation = jnp.clip(1.0 * jax.random.uniform(part_keys[4], (NE, NBLK, NORB), jnp.float32) ** levels(part_keys[4], (NE, NBLK, NORB), ((0, 8), (1, 2)), -0.2, 0.2), 0.0, 1.0)
    return {"ham_diag": ham_diag, "ham_coupling": ham_coupling, "sigma_shift": sigma_shift, "sigma_width": sigma_width, "occupation": occupation}


def matmul(left, right):
    return jnp.einsum('...ij,...jk->...ik', left, right, precision=lax.Precision.HIGHEST)

def cmul(left, right):
    left_re, left_im = (left[..., 0, :, :], left[..., 1, :, :])
    right_re, right_im = (right[..., 0, :, :], right[..., 1, :, :])
    return jnp.stack([matmul(left_re, right_re) - matmul(left_im, right_im), matmul(left_re, right_im) + matmul(left_im, right_re)], axis=-3)

def adjoint(value):
    return jnp.stack([jnp.swapaxes(value[..., 0, :, :], -1, -2), -jnp.swapaxes(value[..., 1, :, :], -1, -2)], axis=-3)

def invert(value):
    real_part = value[..., 0, :, :]
    imag_part = value[..., 1, :, :]
    normal = cmul(adjoint(value), value)
    upper = jnp.concatenate([normal[..., 0, :, :], -normal[..., 1, :, :]], axis=-1)
    lower = jnp.concatenate([normal[..., 1, :, :], normal[..., 0, :, :]], axis=-1)
    factor = jnp.linalg.cholesky(jnp.concatenate([upper, lower], axis=-2))
    target = jnp.concatenate([jnp.swapaxes(real_part, -1, -2), -jnp.swapaxes(imag_part, -1, -2)], axis=-2)
    middle = lax.linalg.triangular_solve(factor, target, left_side=True, lower=True)
    solved = lax.linalg.triangular_solve(factor, middle, left_side=True, lower=True, transpose_a=True)
    order = real_part.shape[-1]
    return jnp.stack([solved[..., :order, :], solved[..., order:, :]], axis=-3)

def sandwich(outer, inner):
    return cmul(cmul(outer, inner), adjoint(outer))

def add_imag_diagonal(matrix, values):
    identity = jnp.eye(values.shape[-1], dtype=jnp.float32)
    extra = jnp.stack([jnp.zeros_like(matrix[..., 0, :, :]), values[..., :, None] * identity], axis=-3)
    return matrix + extra

def reference(ham_diag, ham_coupling, sigma_shift, sigma_width, occupation):
    order = ham_diag.shape[-1]
    energy = -2.0 + 4.0 * (jnp.arange(NE).astype(jnp.float32) + 0.5) / NE
    identity = jnp.eye(order, dtype=jnp.float32)
    real_part = energy[:, None, None, None] * identity - ham_diag[None, :, 0] - sigma_shift[..., :, None] * identity
    imag_part = sigma_width[..., :, None] * identity - ham_diag[None, :, 1]
    system = jnp.stack([real_part, imag_part], axis=2)
    source = 2.0 * occupation * sigma_width
    left_sig = []
    left_less = []
    for block in range(NBLK):
        diagonal = system[:, block]
        if block == 0:
            coupled = jnp.zeros_like(diagonal)
            coupled_less = jnp.zeros_like(diagonal)
        else:
            link = adjoint(ham_coupling[block - 1])
            coupled = sandwich(link, green)
            coupled_less = sandwich(link, green_less)
        green = invert(diagonal - coupled)
        green_less = sandwich(green, add_imag_diagonal(coupled_less, source[:, block]))
        left_sig.append(coupled)
        left_less.append(coupled_less)
    right_sig = [None] * NBLK
    right_less = [None] * NBLK
    for block in reversed(range(NBLK)):
        diagonal = system[:, block]
        if block == NBLK - 1:
            coupled = jnp.zeros_like(diagonal)
            coupled_less = jnp.zeros_like(diagonal)
        else:
            link = ham_coupling[block]
            coupled = sandwich(link, rgreen)
            coupled_less = sandwich(link, rgreen_less)
        rgreen = invert(diagonal - coupled)
        rgreen_less = sandwich(rgreen, add_imag_diagonal(coupled_less, source[:, block]))
        right_sig[block] = coupled
        right_less[block] = coupled_less
    retarded = []
    lesser = []
    for block in range(NBLK):
        diagonal = system[:, block]
        full = invert(diagonal - left_sig[block] - right_sig[block])
        full_less = sandwich(full, add_imag_diagonal(left_less[block] + right_less[block], source[:, block]))
        retarded.append(full)
        lesser.append(full_less)
    retarded = jnp.stack(retarded, axis=1)
    lesser = jnp.stack(lesser, axis=1)
    greater = lesser + retarded - adjoint(retarded)
    a_re, a_im = (lesser[:, :, 0], lesser[:, :, 1])
    b_re, b_im = (greater[:, :, 0], greater[:, :, 1])
    corr_re = []
    corr_im = []
    for shift in range(NE):
        upper_re, upper_im = (a_re[shift:], a_im[shift:])
        lower_re, lower_im = (b_re[:NE - shift], b_im[:NE - shift])
        corr_re.append(jnp.sum(upper_re * lower_re + upper_im * lower_im, axis=0))
        corr_im.append(jnp.sum(upper_im * lower_re - upper_re * lower_im, axis=0))
    corr_re = jnp.stack(corr_re, axis=0)
    corr_im = jnp.stack(corr_im, axis=0)
    return jnp.stack([-order * corr_im, order * corr_re], axis=2)
```

```python
import jax
import jax.numpy as jnp
from jax import lax
from jax.sharding import PartitionSpec as P


def from_partner(shard, axis, distance):
    return lax.ppermute(shard, axis, [(i, i ^ 1 << distance) for i in range(lax.axis_size(axis))])


def dot(left, right, precision=lax.Precision.HIGHEST):
    return jnp.einsum("...ij,...jk->...ik", left, right, precision=precision)


def swap(value):
    return jnp.swapaxes(value, -1, -2)


def embed(real, imag):
    top = jnp.concatenate([real, -imag], axis=-1)
    bottom = jnp.concatenate([imag, real], axis=-1)
    return jnp.concatenate([top, bottom], axis=-2)


def stack(real, imag):
    return jnp.concatenate([real, imag], axis=-2)


def split(stacked):
    order = stacked.shape[-2] // 2
    return stacked[..., :order, :], stacked[..., order:, :]


def stacked_adjoint(real, imag):
    return stack(swap(real), -swap(imag))


def invert(matrix):
    size = matrix.shape[-1]
    eye = jnp.eye(size, dtype=jnp.float32)
    high = lax.Precision.HIGH
    transposed = swap(matrix)
    normal = dot(transposed, matrix, high)
    beta = jnp.max(jnp.sum(jnp.abs(normal), axis=-1), axis=-1) * 1.01 + 1e-30
    beta = beta[..., None, None]
    approx = transposed / beta
    lower = 0.25 / beta
    for _ in range(6):
        alpha = 2.0 / (lower + 1.0)
        product = dot(matrix, approx, high)
        approx = dot(alpha * approx, 2.0 * eye - alpha * product, high)
        ratio = (1.0 - lower) / (1.0 + lower)
        lower = 1.0 - ratio * ratio

    def keep_going(state):
        _, residual, count = state
        return (residual > 1e-3) & (count < 40)

    def newton(state):
        approx, _, count = state
        rest = eye - dot(matrix, approx)
        residual = jnp.sqrt(jnp.max(jnp.sum(rest * rest, axis=(-1, -2))))
        return approx + dot(approx, rest), residual, count + 1

    approx, _, _ = lax.while_loop(
        keep_going, newton, (approx, jnp.float32(jnp.inf), jnp.int32(0))
    )
    return approx


def body(ham_diag, ham_coupling, sigma_shift, sigma_width, occupation):
    blocks = ham_diag.shape[0]
    assert blocks == 1
    energies_here = sigma_shift.shape[0]
    order = ham_diag.shape[-1]
    side = lax.axis_index("space")
    first = side == 0
    total = energies_here * lax.axis_size("energy")
    offset = lax.axis_index("energy") * energies_here
    energy = -2.0 + 4.0 * ((offset + jnp.arange(energies_here)).astype(jnp.float32) + 0.5) / total
    identity = jnp.eye(order, dtype=jnp.float32)
    shift = sigma_shift[:, 0]
    width = sigma_width[:, 0]
    source = 2.0 * occupation[:, 0] * width
    real_part = (
        energy[:, None, None] * identity
        - ham_diag[None, 0, 0]
        - shift[:, :, None] * identity
    )
    imag_part = width[:, :, None] * identity - ham_diag[None, 0, 1]
    system = embed(real_part, imag_part)

    green = invert(system)
    green_col = green[..., :order]
    g_re, g_im = split(green_col)
    scaled = jnp.concatenate(
        [green[..., order:] * source[:, None, :], -green[..., :order] * source[:, None, :]],
        axis=-1,
    )
    green_less = dot(scaled, stacked_adjoint(g_re, g_im))

    far_green, far_less = from_partner((green_col, green_less), "space", 0)

    link = ham_coupling[0]
    link_re = jnp.where(first, link[0], swap(link[0]))
    link_im = jnp.where(first, link[1], -swap(link[1]))
    link_embed = embed(link_re, link_im)
    link_adj = stacked_adjoint(link_re, link_im)
    left = dot(link_embed, jnp.concatenate([far_green, far_less], axis=-1))
    left_green, left_less = left[..., :order], left[..., order:]
    both = jnp.concatenate([embed(*split(left_green)), embed(*split(left_less))], axis=-2)
    coupled = dot(both, link_adj)
    coupled_green = coupled[..., : 2 * order, :]
    coupled_less = coupled[..., 2 * order :, :]

    full = invert(system - embed(*split(coupled_green)))
    full_re, full_im = split(full[..., :order])
    less_re, less_im = split(coupled_less)
    less_im = less_im + source[:, :, None] * identity
    inner = dot(full, stack(less_re, less_im))
    lesser = dot(embed(*split(inner)), stacked_adjoint(full_re, full_im))
    lesser_re, lesser_im = split(lesser)
    greater_re = lesser_re + full_re - swap(full_re)
    greater_im = lesser_im + full_im + swap(full_im)

    paired = jnp.stack(
        [jnp.stack([lesser_re, lesser_im], axis=1), jnp.stack([greater_re, greater_im], axis=1)],
        axis=1,
    )
    arrived = lax.all_to_all(paired, ("energy", "space"), split_axis=3, concat_axis=0, tiled=True)
    row_count = arrived.shape[3]
    arrived = arrived.reshape(
        (lax.axis_size("energy"), lax.axis_size("space"), energies_here, 2, 2, row_count, order)
    )
    arrived = jnp.transpose(arrived, (0, 2, 1, 3, 4, 5, 6))
    regrouped = arrived.reshape((total, lax.axis_size("space"), 2, 2, row_count, order))
    a_re, a_im = regrouped[:, :, 0, 0], regrouped[:, :, 0, 1]
    b_re, b_im = regrouped[:, :, 1, 0], regrouped[:, :, 1, 1]
    corr_re = []
    corr_im = []
    for shift_index in range(total):
        upper_re, upper_im = a_re[shift_index:], a_im[shift_index:]
        lower_re, lower_im = b_re[: total - shift_index], b_im[: total - shift_index]
        corr_re.append(jnp.sum(upper_re * lower_re + upper_im * lower_im, axis=0))
        corr_im.append(jnp.sum(upper_im * lower_re - upper_re * lower_im, axis=0))
    corr_re = jnp.stack(corr_re, axis=0)
    corr_im = jnp.stack(corr_im, axis=0)
    return jnp.stack([-order * corr_im, order * corr_re], axis=2)


def solution(mesh):
    return jax.shard_map(
        body,
        mesh=mesh,
        in_specs=(
            P("space", None, "groups", None),
            P("groups", None, None, None),
            P("energy", "space", "groups"),
            P("energy", "space", "groups"),
            P("energy", "space", "groups"),
        ),
        out_specs=P("groups", None, None, ("energy", "space"), None),
        check_vma=False,
    )
```

```python
import jax
import jax.numpy as jnp
from jax import lax
from jax.sharding import PartitionSpec as P


def from_partner(shard, axis, distance):
    return lax.ppermute(shard, axis, [(i, i ^ 1 << distance) for i in range(lax.axis_size(axis))])


def dot(left, right, precision=lax.Precision.HIGHEST):
    return jnp.einsum("...ij,...jk->...ik", left, right, precision=precision)


def swap(value):
    return jnp.swapaxes(value, -1, -2)


def embed(real, imag):
    top = jnp.concatenate([real, -imag], axis=-1)
    bottom = jnp.concatenate([imag, real], axis=-1)
    return jnp.concatenate([top, bottom], axis=-2)


def stack(real, imag):
    return jnp.concatenate([real, imag], axis=-2)


def split(stacked):
    order = stacked.shape[-2] // 2
    return stacked[..., :order, :], stacked[..., order:, :]


def stacked_adjoint(real, imag):
    return stack(swap(real), -swap(imag))


def invert(matrix):
    size = matrix.shape[-1]
    eye = jnp.eye(size, dtype=jnp.float32)
    high = lax.Precision.HIGH
    transposed = swap(matrix)
    normal = dot(transposed, matrix, high)
    square = dot(normal, normal, high)
    beta = jnp.sqrt(jnp.max(jnp.sum(jnp.abs(square), axis=-1), axis=-1)) * 1.01 + 1e-30
    beta = beta[..., None, None]
    approx = transposed / beta
    lower = 0.25 / beta
    for _ in range(7):
        alpha = 2.0 / (lower + 1.0)
        product = dot(matrix, approx, high)
        approx = dot(alpha * approx, 2.0 * eye - alpha * product, high)
        ratio = (1.0 - lower) / (1.0 + lower)
        lower = 1.0 - ratio * ratio

    def keep_going(state):
        _, residual, count = state
        return (residual > 1e-3) & (count < 40)

    def newton(state):
        approx, _, count = state
        rest = eye - dot(matrix, approx)
        residual = jnp.sqrt(jnp.max(jnp.sum(rest * rest, axis=(-1, -2))))
        return approx + dot(approx, rest, high), residual, count + 1

    approx, _, _ = lax.while_loop(
        keep_going, newton, (approx, jnp.float32(jnp.inf), jnp.int32(0))
    )
    return approx


def body(ham_diag, ham_coupling, sigma_shift, sigma_width, occupation):
    blocks = ham_diag.shape[0]
    assert blocks == 1
    energies_here = sigma_shift.shape[0]
    order = ham_diag.shape[-1]
    side = lax.axis_index("space")
    first = side == 0
    total = energies_here * lax.axis_size("energy")
    offset = lax.axis_index("energy") * energies_here
    energy = -2.0 + 4.0 * ((offset + jnp.arange(energies_here)).astype(jnp.float32) + 0.5) / total
    identity = jnp.eye(order, dtype=jnp.float32)
    shift = sigma_shift[:, 0]
    width = sigma_width[:, 0]
    source = 2.0 * occupation[:, 0] * width
    real_part = (
        energy[:, None, None] * identity
        - ham_diag[None, 0, 0]
        - shift[:, :, None] * identity
    )
    imag_part = width[:, :, None] * identity - ham_diag[None, 0, 1]
    system = embed(real_part, imag_part)

    green = invert(system)
    green_col = green[..., :order]
    g_re, g_im = split(green_col)
    scaled = jnp.concatenate(
        [green[..., order:] * source[:, None, :], -green[..., :order] * source[:, None, :]],
        axis=-1,
    )
    green_less = dot(scaled, stacked_adjoint(g_re, g_im))

    far_green, far_less = from_partner((green_col, green_less), "space", 0)

    link = ham_coupling[0]
    link_re = jnp.where(first, link[0], swap(link[0]))
    link_im = jnp.where(first, link[1], -swap(link[1]))
    link_embed = embed(link_re, link_im)
    link_adj = stacked_adjoint(link_re, link_im)
    left = dot(link_embed, jnp.concatenate([far_green, far_less], axis=-1))
    left_green, left_less = left[..., :order], left[..., order:]
    both = jnp.concatenate([embed(*split(left_green)), embed(*split(left_less))], axis=-2)
    coupled = dot(both, link_adj)
    coupled_green = coupled[..., : 2 * order, :]
    coupled_less = coupled[..., 2 * order :, :]

    full = invert(system - embed(*split(coupled_green)))
    full_re, full_im = split(full[..., :order])
    less_re, less_im = split(coupled_less)
    less_im = less_im + source[:, :, None] * identity
    inner = dot(full, stack(less_re, less_im))
    lesser = dot(embed(*split(inner)), stacked_adjoint(full_re, full_im))
    lesser_re, lesser_im = split(lesser)
    greater_re = lesser_re + full_re - swap(full_re)
    greater_im = lesser_im + full_im + swap(full_im)

    paired = jnp.stack(
        [jnp.stack([lesser_re, lesser_im], axis=1), jnp.stack([greater_re, greater_im], axis=1)],
        axis=1,
    )
    arrived = lax.all_to_all(paired, ("energy", "space"), split_axis=3, concat_axis=0, tiled=True)
    row_count = arrived.shape[3]
    arrived = arrived.reshape(
        (lax.axis_size("energy"), lax.axis_size("space"), energies_here, 2, 2, row_count, order)
    )
    arrived = jnp.transpose(arrived, (0, 2, 1, 3, 4, 5, 6))
    regrouped = arrived.reshape((total, lax.axis_size("space"), 2, 2, row_count, order))
    a_re, a_im = regrouped[:, :, 0, 0], regrouped[:, :, 0, 1]
    b_re, b_im = regrouped[:, :, 1, 0], regrouped[:, :, 1, 1]
    corr_re = []
    corr_im = []
    for shift_index in range(total):
        upper_re, upper_im = a_re[shift_index:], a_im[shift_index:]
        lower_re, lower_im = b_re[: total - shift_index], b_im[: total - shift_index]
        corr_re.append(jnp.sum(upper_re * lower_re + upper_im * lower_im, axis=0))
        corr_im.append(jnp.sum(upper_im * lower_re - upper_re * lower_im, axis=0))
    corr_re = jnp.stack(corr_re, axis=0)
    corr_im = jnp.stack(corr_im, axis=0)
    return jnp.stack([-order * corr_im, order * corr_re], axis=2)


def solution(mesh):
    return jax.shard_map(
        body,
        mesh=mesh,
        in_specs=(
            P("space", None, "groups", None),
            P("groups", None, None, None),
            P("energy", "space", "groups"),
            P("energy", "space", "groups"),
            P("energy", "space", "groups"),
        ),
        out_specs=P("groups", None, None, ("energy", "space"), None),
        check_vma=False,
    )
```

```python
import jax
import jax.numpy as jnp
from jax import lax
from jax.sharding import PartitionSpec as P


def from_partner(shard, axis, distance):
    return lax.ppermute(shard, axis, [(i, i ^ 1 << distance) for i in range(lax.axis_size(axis))])


def dot(left, right, precision=lax.Precision.HIGHEST):
    return jnp.einsum("...ij,...jk->...ik", left, right, precision=precision)


def swap(value):
    return jnp.swapaxes(value, -1, -2)


def embed(real, imag):
    top = jnp.concatenate([real, -imag], axis=-1)
    bottom = jnp.concatenate([imag, real], axis=-1)
    return jnp.concatenate([top, bottom], axis=-2)


def stack(real, imag):
    return jnp.concatenate([real, imag], axis=-2)


def split(stacked):
    order = stacked.shape[-2] // 2
    return stacked[..., :order, :], stacked[..., order:, :]


def stacked_adjoint(real, imag):
    return stack(swap(real), -swap(imag))


def invert(matrix):
    order = matrix.shape[-1] // 2
    eye = stack(jnp.eye(order, dtype=jnp.float32), jnp.zeros((order, order), jnp.float32))
    high = lax.Precision.HIGH
    transposed = swap(matrix)
    normal = dot(transposed, matrix[..., :order], high)
    square = dot(embed(*split(normal)), normal, high)
    square_re, square_im = split(square)
    rows = jnp.sum(jnp.abs(square_re) + jnp.abs(square_im), axis=-1)
    beta = jnp.sqrt(jnp.max(rows, axis=-1)) * 1.01 + 1e-30
    beta = beta[..., None, None]
    approx = transposed[..., :order] / beta
    lower = 0.25 / beta
    for _ in range(7):
        alpha = 2.0 / (lower + 1.0)
        product = dot(matrix, approx, high)
        approx = dot(alpha * embed(*split(approx)), 2.0 * eye - alpha * product, high)
        ratio = (1.0 - lower) / (1.0 + lower)
        lower = 1.0 - ratio * ratio

    def keep_going(state):
        _, residual, count = state
        return (residual > 7e-4) & (count < 40)

    def newton(state):
        approx, _, count = state
        rest = eye - dot(matrix, approx)
        residual = jnp.sqrt(jnp.max(jnp.sum(rest * rest, axis=(-1, -2))))
        return approx + dot(embed(*split(approx)), rest, high), residual, count + 1

    approx, _, _ = lax.while_loop(
        keep_going, newton, (approx, jnp.float32(jnp.inf), jnp.int32(0))
    )
    return approx


def body(ham_diag, ham_coupling, sigma_shift, sigma_width, occupation):
    blocks = ham_diag.shape[0]
    assert blocks == 1
    energies_here = sigma_shift.shape[0]
    order = ham_diag.shape[-1]
    side = lax.axis_index("space")
    first = side == 0
    total = energies_here * lax.axis_size("energy")
    offset = lax.axis_index("energy") * energies_here
    energy = -2.0 + 4.0 * ((offset + jnp.arange(energies_here)).astype(jnp.float32) + 0.5) / total
    identity = jnp.eye(order, dtype=jnp.float32)
    shift = sigma_shift[:, 0]
    width = sigma_width[:, 0]
    source = 2.0 * occupation[:, 0] * width
    real_part = (
        energy[:, None, None] * identity
        - ham_diag[None, 0, 0]
        - shift[:, :, None] * identity
    )
    imag_part = width[:, :, None] * identity - ham_diag[None, 0, 1]
    system = embed(real_part, imag_part)

    green_col = invert(system)
    g_re, g_im = split(green_col)
    scaled = embed(-g_im * source[:, None, :], g_re * source[:, None, :])
    green_less = dot(scaled, stacked_adjoint(g_re, g_im))

    far_green, far_less = from_partner((green_col, green_less), "space", 0)

    link = ham_coupling[0]
    link_re = jnp.where(first, link[0], swap(link[0]))
    link_im = jnp.where(first, link[1], -swap(link[1]))
    link_embed = embed(link_re, link_im)
    link_adj = stacked_adjoint(link_re, link_im)
    left = dot(link_embed, jnp.concatenate([far_green, far_less], axis=-1))
    left_green, left_less = left[..., :order], left[..., order:]
    both = jnp.concatenate([embed(*split(left_green)), embed(*split(left_less))], axis=-2)
    coupled = dot(both, link_adj)
    coupled_green = coupled[..., : 2 * order, :]
    coupled_less = coupled[..., 2 * order :, :]

    full_re, full_im = split(invert(system - embed(*split(coupled_green))))
    less_re, less_im = split(coupled_less)
    less_im = less_im + source[:, :, None] * identity
    inner = dot(embed(full_re, full_im), stack(less_re, less_im))
    lesser = dot(embed(*split(inner)), stacked_adjoint(full_re, full_im))
    lesser_re, lesser_im = split(lesser)
    greater_re = lesser_re + full_re - swap(full_re)
    greater_im = lesser_im + full_im + swap(full_im)

    paired = jnp.stack(
        [jnp.stack([lesser_re, lesser_im], axis=1), jnp.stack([greater_re, greater_im], axis=1)],
        axis=1,
    )
    arrived = lax.all_to_all(paired, ("energy", "space"), split_axis=3, concat_axis=0, tiled=True)
    row_count = arrived.shape[3]
    arrived = arrived.reshape(
        (lax.axis_size("energy"), lax.axis_size("space"), energies_here, 2, 2, row_count, order)
    )
    arrived = jnp.transpose(arrived, (0, 2, 1, 3, 4, 5, 6))
    regrouped = arrived.reshape((total, lax.axis_size("space"), 2, 2, row_count, order))
    a_re, a_im = regrouped[:, :, 0, 0], regrouped[:, :, 0, 1]
    b_re, b_im = regrouped[:, :, 1, 0], regrouped[:, :, 1, 1]
    corr_re = []
    corr_im = []
    for shift_index in range(total):
        upper_re, upper_im = a_re[shift_index:], a_im[shift_index:]
        lower_re, lower_im = b_re[: total - shift_index], b_im[: total - shift_index]
        corr_re.append(jnp.sum(upper_re * lower_re + upper_im * lower_im, axis=0))
        corr_im.append(jnp.sum(upper_im * lower_re - upper_re * lower_im, axis=0))
    corr_re = jnp.stack(corr_re, axis=0)
    corr_im = jnp.stack(corr_im, axis=0)
    return jnp.stack([-order * corr_im, order * corr_re], axis=2)


def solution(mesh):
    return jax.shard_map(
        body,
        mesh=mesh,
        in_specs=(
            P("space", None, "groups", None),
            P("groups", None, None, None),
            P("energy", "space", "groups"),
            P("energy", "space", "groups"),
            P("energy", "space", "groups"),
        ),
        out_specs=P("groups", None, None, ("energy", "space"), None),
        check_vma=False,
    )
```

```python
import jax
import jax.numpy as jnp
from jax import lax
from jax.sharding import PartitionSpec as P


def from_partner(shard, axis, distance):
    return lax.ppermute(shard, axis, [(i, i ^ 1 << distance) for i in range(lax.axis_size(axis))])


def dot(left, right, precision=lax.Precision.HIGHEST):
    return jnp.einsum("...ij,...jk->...ik", left, right, precision=precision)


def swap(value):
    return jnp.swapaxes(value, -1, -2)


def embed(real, imag):
    top = jnp.concatenate([real, -imag], axis=-1)
    bottom = jnp.concatenate([imag, real], axis=-1)
    return jnp.concatenate([top, bottom], axis=-2)


def stack(real, imag):
    return jnp.concatenate([real, imag], axis=-2)


def split(stacked):
    order = stacked.shape[-2] // 2
    return stacked[..., :order, :], stacked[..., order:, :]


def stacked_adjoint(real, imag):
    return stack(swap(real), -swap(imag))


def invert(matrix):
    order = matrix.shape[-1] // 2
    eye = stack(jnp.eye(order, dtype=jnp.float32), jnp.zeros((order, order), jnp.float32))
    high = lax.Precision.HIGH
    transposed = swap(matrix)
    normal = dot(transposed, matrix[..., :order], high)
    square = dot(embed(*split(normal)), normal, high)
    square_re, square_im = split(square)
    rows = jnp.sum(jnp.abs(square_re) + jnp.abs(square_im), axis=-1)
    beta = jnp.sqrt(jnp.max(rows, axis=-1)) * 1.01 + 1e-30
    beta = beta[..., None, None]
    approx = transposed[..., :order] / beta
    lower = 0.25 / beta
    for _ in range(7):
        alpha = 2.0 / (lower + 1.0)
        product = dot(matrix, approx, high)
        approx = dot(alpha * embed(*split(approx)), 2.0 * eye - alpha * product, high)
        ratio = (1.0 - lower) / (1.0 + lower)
        lower = 1.0 - ratio * ratio

    def keep_going(state):
        _, residual, count = state
        return (residual > 7e-4) & (count < 40)

    def newton(state):
        approx, _, count = state
        rest = eye - dot(matrix, approx)
        residual = jnp.sqrt(jnp.max(jnp.sum(rest * rest, axis=(-1, -2))))
        return approx + dot(embed(*split(approx)), rest, high), residual, count + 1

    approx, _, _ = lax.while_loop(
        keep_going, newton, (approx, jnp.float32(jnp.inf), jnp.int32(0))
    )
    return approx


def body(ham_diag, ham_coupling, sigma_shift, sigma_width, occupation):
    blocks = ham_diag.shape[0]
    assert blocks == 1
    energies_here = sigma_shift.shape[0]
    order = ham_diag.shape[-1]
    side = lax.axis_index("space")
    first = side == 0
    total = energies_here * lax.axis_size("energy")
    offset = lax.axis_index("energy") * energies_here
    energy = -2.0 + 4.0 * ((offset + jnp.arange(energies_here)).astype(jnp.float32) + 0.5) / total
    identity = jnp.eye(order, dtype=jnp.float32)
    shift = sigma_shift[:, 0]
    width = sigma_width[:, 0]
    source = 2.0 * occupation[:, 0] * width
    real_part = (
        energy[:, None, None] * identity
        - ham_diag[None, 0, 0]
        - shift[:, :, None] * identity
    )
    imag_part = width[:, :, None] * identity - ham_diag[None, 0, 1]
    system = embed(real_part, imag_part)

    green_col = invert(system)
    g_re, g_im = split(green_col)
    scaled = embed(-g_im * source[:, None, :], g_re * source[:, None, :])
    green_less = dot(scaled, stacked_adjoint(g_re, g_im))

    far_green, far_less = from_partner((green_col, green_less), "space", 0)

    link = ham_coupling[0]
    link_re = jnp.where(first, link[0], swap(link[0]))
    link_im = jnp.where(first, link[1], -swap(link[1]))
    link_embed = embed(link_re, link_im)
    link_adj = stacked_adjoint(link_re, link_im)
    left = dot(link_embed, jnp.concatenate([far_green, far_less], axis=-1), lax.Precision.HIGH)
    left_green, left_less = left[..., :order], left[..., order:]
    both = jnp.concatenate([embed(*split(left_green)), embed(*split(left_less))], axis=-2)
    coupled = dot(both, link_adj, lax.Precision.HIGH)
    coupled_green = coupled[..., : 2 * order, :]
    coupled_less = coupled[..., 2 * order :, :]

    full_re, full_im = split(invert(system - embed(*split(coupled_green))))
    less_re, less_im = split(coupled_less)
    less_im = less_im + source[:, :, None] * identity
    inner = dot(embed(full_re, full_im), stack(less_re, less_im))
    lesser = dot(embed(*split(inner)), stacked_adjoint(full_re, full_im))
    lesser_re, lesser_im = split(lesser)
    greater_re = lesser_re + full_re - swap(full_re)
    greater_im = lesser_im + full_im + swap(full_im)

    paired = jnp.stack(
        [jnp.stack([lesser_re, lesser_im], axis=1), jnp.stack([greater_re, greater_im], axis=1)],
        axis=1,
    )
    arrived = lax.all_to_all(paired, ("energy", "space"), split_axis=3, concat_axis=0, tiled=True)
    row_count = arrived.shape[3]
    arrived = arrived.reshape(
        (lax.axis_size("energy"), lax.axis_size("space"), energies_here, 2, 2, row_count, order)
    )
    arrived = jnp.transpose(arrived, (0, 2, 1, 3, 4, 5, 6))
    regrouped = arrived.reshape((total, lax.axis_size("space"), 2, 2, row_count, order))
    a_re, a_im = regrouped[:, :, 0, 0], regrouped[:, :, 0, 1]
    b_re, b_im = regrouped[:, :, 1, 0], regrouped[:, :, 1, 1]
    corr_re = []
    corr_im = []
    for shift_index in range(total):
        upper_re, upper_im = a_re[shift_index:], a_im[shift_index:]
        lower_re, lower_im = b_re[: total - shift_index], b_im[: total - shift_index]
        corr_re.append(jnp.sum(upper_re * lower_re + upper_im * lower_im, axis=0))
        corr_im.append(jnp.sum(upper_im * lower_re - upper_re * lower_im, axis=0))
    corr_re = jnp.stack(corr_re, axis=0)
    corr_im = jnp.stack(corr_im, axis=0)
    return jnp.stack([-order * corr_im, order * corr_re], axis=2)


def solution(mesh):
    return jax.shard_map(
        body,
        mesh=mesh,
        in_specs=(
            P("space", None, "groups", None),
            P("groups", None, None, None),
            P("energy", "space", "groups"),
            P("energy", "space", "groups"),
            P("energy", "space", "groups"),
        ),
        out_specs=P("groups", None, None, ("energy", "space"), None),
        check_vma=False,
    )
```

```python
import jax
import jax.numpy as jnp
from jax import lax
from jax.sharding import PartitionSpec as P


def from_partner(shard, axis, distance):
    return lax.ppermute(shard, axis, [(i, i ^ 1 << distance) for i in range(lax.axis_size(axis))])


def dot(left, right, precision=lax.Precision.HIGHEST):
    return jnp.einsum("...ij,...jk->...ik", left, right, precision=precision)


def swap(value):
    return jnp.swapaxes(value, -1, -2)


def embed(real, imag):
    top = jnp.concatenate([real, -imag], axis=-1)
    bottom = jnp.concatenate([imag, real], axis=-1)
    return jnp.concatenate([top, bottom], axis=-2)


def stack(real, imag):
    return jnp.concatenate([real, imag], axis=-2)


def split(stacked):
    order = stacked.shape[-2] // 2
    return stacked[..., :order, :], stacked[..., order:, :]


def stacked_adjoint(real, imag):
    return stack(swap(real), -swap(imag))


def invert(matrix):
    order = matrix.shape[-1] // 2
    eye = stack(jnp.eye(order, dtype=jnp.float32), jnp.zeros((order, order), jnp.float32))
    high = lax.Precision.HIGH
    transposed = swap(matrix)
    normal = dot(transposed, matrix[..., :order], high)
    square = dot(embed(*split(normal)), normal, high)
    square_re, square_im = split(square)
    rows = jnp.sum(jnp.abs(square_re) + jnp.abs(square_im), axis=-1)
    beta = jnp.sqrt(jnp.max(rows, axis=-1)) * 1.01 + 1e-30
    beta = beta[..., None, None]
    approx = transposed[..., :order] / beta
    lower = 0.25 / beta
    for _ in range(7):
        alpha = 2.0 / (lower + 1.0)
        product = dot(matrix, approx, high)
        approx = dot(alpha * embed(*split(approx)), 2.0 * eye - alpha * product, high)
        ratio = (1.0 - lower) / (1.0 + lower)
        lower = 1.0 - ratio * ratio

    def keep_going(state):
        _, residual, count = state
        return (residual > 7e-4) & (count < 40)

    def newton(state):
        approx, _, count = state
        rest = eye - dot(matrix, approx)
        residual = jnp.sqrt(jnp.max(jnp.sum(rest * rest, axis=(-1, -2))))
        return approx + dot(embed(*split(approx)), rest, high), residual, count + 1

    approx, _, _ = lax.while_loop(
        keep_going, newton, (approx, jnp.float32(jnp.inf), jnp.int32(0))
    )
    return approx


def body(ham_diag, ham_coupling, sigma_shift, sigma_width, occupation):
    blocks = ham_diag.shape[0]
    assert blocks == 1
    energies_here = sigma_shift.shape[0]
    order = ham_diag.shape[-1]
    side = lax.axis_index("space")
    first = side == 0
    total = energies_here * lax.axis_size("energy")
    offset = lax.axis_index("energy") * energies_here
    energy = -2.0 + 4.0 * ((offset + jnp.arange(energies_here)).astype(jnp.float32) + 0.5) / total
    identity = jnp.eye(order, dtype=jnp.float32)
    shift = sigma_shift[:, 0]
    width = sigma_width[:, 0]
    source = 2.0 * occupation[:, 0] * width
    real_part = (
        energy[:, None, None] * identity
        - ham_diag[None, 0, 0]
        - shift[:, :, None] * identity
    )
    imag_part = width[:, :, None] * identity - ham_diag[None, 0, 1]
    system = embed(real_part, imag_part)

    green_col = invert(system)
    g_re, g_im = split(green_col)
    scaled = embed(-g_im * source[:, None, :], g_re * source[:, None, :])
    far_green = from_partner(green_col, "space", 0)
    green_less = dot(scaled, stacked_adjoint(g_re, g_im))
    far_less = from_partner(green_less, "space", 0)

    link = ham_coupling[0]
    link_re = jnp.where(first, link[0], swap(link[0]))
    link_im = jnp.where(first, link[1], -swap(link[1]))
    link_embed = embed(link_re, link_im)
    link_adj = stacked_adjoint(link_re, link_im)
    high = lax.Precision.HIGH
    left_green = dot(link_embed, far_green, high)
    coupled_green = dot(embed(*split(left_green)), link_adj, high)
    left_less = dot(link_embed, far_less, high)
    coupled_less = dot(embed(*split(left_less)), link_adj, high)

    full_re, full_im = split(invert(system - embed(*split(coupled_green))))
    less_re, less_im = split(coupled_less)
    less_im = less_im + source[:, :, None] * identity
    inner = dot(embed(full_re, full_im), stack(less_re, less_im))
    lesser = dot(embed(*split(inner)), stacked_adjoint(full_re, full_im))
    lesser_re, lesser_im = split(lesser)
    greater_re = lesser_re + full_re - swap(full_re)
    greater_im = lesser_im + full_im + swap(full_im)

    chunks = lax.axis_size("energy") * lax.axis_size("space")
    row_count = order // chunks
    parts = [lesser_re, lesser_im, greater_re, greater_im]
    parts = [part.reshape((energies_here, chunks, row_count, order)) for part in parts]
    paired = jnp.moveaxis(jnp.stack(parts, axis=2), 1, 0)
    arrived = lax.all_to_all(paired, ("energy", "space"), split_axis=0, concat_axis=0, tiled=True)
    arrived = arrived.reshape(
        (lax.axis_size("energy"), lax.axis_size("space"), energies_here, 4, row_count, order)
    )
    arrived = jnp.transpose(arrived, (0, 2, 1, 3, 4, 5))
    regrouped = arrived.reshape((total, lax.axis_size("space"), 2, 2, row_count, order))
    a_re, a_im = regrouped[:, :, 0, 0], regrouped[:, :, 0, 1]
    b_re, b_im = regrouped[:, :, 1, 0], regrouped[:, :, 1, 1]
    corr_re = []
    corr_im = []
    for shift_index in range(total):
        upper_re, upper_im = a_re[shift_index:], a_im[shift_index:]
        lower_re, lower_im = b_re[: total - shift_index], b_im[: total - shift_index]
        corr_re.append(jnp.sum(upper_re * lower_re + upper_im * lower_im, axis=0))
        corr_im.append(jnp.sum(upper_im * lower_re - upper_re * lower_im, axis=0))
    corr_re = jnp.stack(corr_re, axis=0)
    corr_im = jnp.stack(corr_im, axis=0)
    return jnp.stack([-order * corr_im, order * corr_re], axis=2)


def solution(mesh):
    return jax.shard_map(
        body,
        mesh=mesh,
        in_specs=(
            P("space", None, "groups", None),
            P("groups", None, None, None),
            P("energy", "space", "groups"),
            P("energy", "space", "groups"),
            P("energy", "space", "groups"),
        ),
        out_specs=P("groups", None, None, ("energy", "space"), None),
        check_vma=False,
    )
```

```python
import jax
import jax.numpy as jnp
from jax import lax
from jax.sharding import PartitionSpec as P


def from_partner(shard, axis, distance):
    return lax.ppermute(shard, axis, [(i, i ^ 1 << distance) for i in range(lax.axis_size(axis))])


def dot(left, right, precision=lax.Precision.HIGHEST):
    return jnp.einsum("...ij,...jk->...ik", left, right, precision=precision)


def swap(value):
    return jnp.swapaxes(value, -1, -2)


def embed(real, imag):
    top = jnp.concatenate([real, -imag], axis=-1)
    bottom = jnp.concatenate([imag, real], axis=-1)
    return jnp.concatenate([top, bottom], axis=-2)


def stack(real, imag):
    return jnp.concatenate([real, imag], axis=-2)


def split(stacked):
    order = stacked.shape[-2] // 2
    return stacked[..., :order, :], stacked[..., order:, :]


def stacked_adjoint(real, imag):
    return stack(swap(real), -swap(imag))


def invert(matrix):
    order = matrix.shape[-1] // 2
    eye = stack(jnp.eye(order, dtype=jnp.float32), jnp.zeros((order, order), jnp.float32))
    high = lax.Precision.HIGH
    gram = jnp.einsum("...ij,...kj->...ik", matrix, matrix[..., :order, :], precision=high)
    square = dot(embed(*split(gram)), gram, high)
    square_re, square_im = split(square)
    rows = jnp.sum(jnp.abs(square_re) + jnp.abs(square_im), axis=-1)
    beta = jnp.sqrt(jnp.max(rows, axis=-1)) * 1.01 + 1e-30
    beta = beta[..., None, None]
    lower = 0.25 / beta
    alpha = 2.0 / (lower + 1.0)
    first_step = 2.0 * eye - (alpha / beta) * gram
    approx = jnp.einsum("...ji,...jk->...ik", matrix, first_step, precision=high) * (alpha / beta)
    ratio = (1.0 - lower) / (1.0 + lower)
    lower = 1.0 - ratio * ratio
    for _ in range(6):
        alpha = 2.0 / (lower + 1.0)
        product = dot(matrix, approx, high)
        approx = dot(alpha * embed(*split(approx)), 2.0 * eye - alpha * product, high)
        ratio = (1.0 - lower) / (1.0 + lower)
        lower = 1.0 - ratio * ratio

    def keep_going(state):
        _, residual, count = state
        return (residual > 7e-4) & (count < 40)

    def newton(state):
        approx, _, count = state
        rest = eye - dot(matrix, approx)
        residual = jnp.sqrt(jnp.max(jnp.sum(rest * rest, axis=(-1, -2))))
        return approx + dot(embed(*split(approx)), rest, high), residual, count + 1

    approx, _, _ = lax.while_loop(
        keep_going, newton, (approx, jnp.float32(jnp.inf), jnp.int32(0))
    )
    return approx


def body(ham_diag, ham_coupling, sigma_shift, sigma_width, occupation):
    blocks = ham_diag.shape[0]
    assert blocks == 1
    energies_here = sigma_shift.shape[0]
    order = ham_diag.shape[-1]
    side = lax.axis_index("space")
    first = side == 0
    total = energies_here * lax.axis_size("energy")
    offset = lax.axis_index("energy") * energies_here
    energy = -2.0 + 4.0 * ((offset + jnp.arange(energies_here)).astype(jnp.float32) + 0.5) / total
    identity = jnp.eye(order, dtype=jnp.float32)
    shift = sigma_shift[:, 0]
    width = sigma_width[:, 0]
    source = 2.0 * occupation[:, 0] * width
    real_part = (
        energy[:, None, None] * identity
        - ham_diag[None, 0, 0]
        - shift[:, :, None] * identity
    )
    imag_part = width[:, :, None] * identity - ham_diag[None, 0, 1]
    system = embed(real_part, imag_part)

    green_col = invert(system)
    g_re, g_im = split(green_col)
    scaled = embed(-g_im * source[:, None, :], g_re * source[:, None, :])
    far_green = from_partner(green_col, "space", 0)
    green_less = dot(scaled, stacked_adjoint(g_re, g_im))
    far_less = from_partner(green_less, "space", 0)

    link = ham_coupling[0]
    link_re = jnp.where(first, link[0], swap(link[0]))
    link_im = jnp.where(first, link[1], -swap(link[1]))
    link_embed = embed(link_re, link_im)
    link_adj = stacked_adjoint(link_re, link_im)
    high = lax.Precision.HIGH
    left_green = dot(link_embed, far_green, high)
    coupled_green = dot(embed(*split(left_green)), link_adj, high)
    left_less = dot(link_embed, far_less, high)
    coupled_less = dot(embed(*split(left_less)), link_adj, high)

    full_re, full_im = split(invert(system - embed(*split(coupled_green))))
    less_re, less_im = split(coupled_less)
    less_im = less_im + source[:, :, None] * identity
    inner = dot(embed(full_re, full_im), stack(less_re, less_im))
    lesser = dot(embed(*split(inner)), stacked_adjoint(full_re, full_im))
    lesser_re, lesser_im = split(lesser)
    greater_re = lesser_re + full_re - swap(full_re)
    greater_im = lesser_im + full_im + swap(full_im)

    chunks = lax.axis_size("energy") * lax.axis_size("space")
    row_count = order // chunks
    parts = [lesser_re, lesser_im, greater_re, greater_im]
    parts = [part.reshape((energies_here, chunks, row_count, order)) for part in parts]
    paired = jnp.moveaxis(jnp.stack(parts, axis=2), 1, 0)
    arrived = lax.all_to_all(paired, ("energy", "space"), split_axis=0, concat_axis=0, tiled=True)
    arrived = arrived.reshape(
        (lax.axis_size("energy"), lax.axis_size("space"), energies_here, 4, row_count, order)
    )
    arrived = jnp.transpose(arrived, (0, 2, 1, 3, 4, 5))
    regrouped = arrived.reshape((total, lax.axis_size("space"), 2, 2, row_count, order))
    a_re, a_im = regrouped[:, :, 0, 0], regrouped[:, :, 0, 1]
    b_re, b_im = regrouped[:, :, 1, 0], regrouped[:, :, 1, 1]
    corr_re = []
    corr_im = []
    for shift_index in range(total):
        upper_re, upper_im = a_re[shift_index:], a_im[shift_index:]
        lower_re, lower_im = b_re[: total - shift_index], b_im[: total - shift_index]
        corr_re.append(jnp.sum(upper_re * lower_re + upper_im * lower_im, axis=0))
        corr_im.append(jnp.sum(upper_im * lower_re - upper_re * lower_im, axis=0))
    corr_re = jnp.stack(corr_re, axis=0)
    corr_im = jnp.stack(corr_im, axis=0)
    return jnp.stack([-order * corr_im, order * corr_re], axis=2)


def solution(mesh):
    return jax.shard_map(
        body,
        mesh=mesh,
        in_specs=(
            P("space", None, "groups", None),
            P("groups", None, None, None),
            P("energy", "space", "groups"),
            P("energy", "space", "groups"),
            P("energy", "space", "groups"),
        ),
        out_specs=P("groups", None, None, ("energy", "space"), None),
        check_vma=False,
    )
```

```python
import jax
import jax.numpy as jnp
from jax import lax
from jax.sharding import PartitionSpec as P


def from_partner(shard, axis, distance):
    return lax.ppermute(shard, axis, [(i, i ^ 1 << distance) for i in range(lax.axis_size(axis))])


def dot(left, right, precision=lax.Precision.HIGHEST):
    return jnp.einsum("...ij,...jk->...ik", left, right, precision=precision)


def swap(value):
    return jnp.swapaxes(value, -1, -2)


def embed(real, imag):
    top = jnp.concatenate([real, -imag], axis=-1)
    bottom = jnp.concatenate([imag, real], axis=-1)
    return jnp.concatenate([top, bottom], axis=-2)


def stack(real, imag):
    return jnp.concatenate([real, imag], axis=-2)


def split(stacked):
    order = stacked.shape[-2] // 2
    return stacked[..., :order, :], stacked[..., order:, :]


def stacked_adjoint(real, imag):
    return stack(swap(real), -swap(imag))


def invert(matrix):
    order = matrix.shape[-1] // 2
    eye = stack(jnp.eye(order, dtype=jnp.float32), jnp.zeros((order, order), jnp.float32))
    high = lax.Precision.HIGH
    gram = jnp.einsum("...ij,...kj->...ik", matrix, matrix[..., :order, :], precision=high)
    square = dot(embed(*split(gram)), gram, high)
    square_re, square_im = split(square)
    rows = jnp.sum(jnp.abs(square_re) + jnp.abs(square_im), axis=-1)
    beta = jnp.sqrt(jnp.max(rows, axis=-1)) * 1.01 + 1e-30
    beta = beta[..., None, None]
    lower = 0.25 / beta
    alpha = 2.0 / (lower + 1.0)
    first_step = 2.0 * eye - (alpha / beta) * gram
    approx = jnp.einsum("...ji,...jk->...ik", matrix, first_step, precision=high) * (alpha / beta)
    ratio = (1.0 - lower) / (1.0 + lower)
    lower = 1.0 - ratio * ratio
    for _ in range(6):
        alpha = 2.0 / (lower + 1.0)
        product = dot(matrix, approx, high)
        approx = dot(alpha * embed(*split(approx)), 2.0 * eye - alpha * product, high)
        ratio = (1.0 - lower) / (1.0 + lower)
        lower = 1.0 - ratio * ratio

    def keep_going(state):
        _, residual, count = state
        return (residual > 7e-4) & (count < 40)

    def newton(state):
        approx, _, count = state
        rest = eye - dot(matrix, approx)
        residual = jnp.sqrt(jnp.max(jnp.sum(rest * rest, axis=(-1, -2))))
        return approx + dot(embed(*split(approx)), rest, high), residual, count + 1

    approx, _, _ = lax.while_loop(
        keep_going, newton, (approx, jnp.float32(jnp.inf), jnp.int32(0))
    )
    return approx


def body(ham_diag, ham_coupling, sigma_shift, sigma_width, occupation):
    blocks = ham_diag.shape[0]
    assert blocks == 1
    energies_here = sigma_shift.shape[0]
    order = ham_diag.shape[-1]
    side = lax.axis_index("space")
    first = side == 0
    total = energies_here * lax.axis_size("energy")
    offset = lax.axis_index("energy") * energies_here
    energy = -2.0 + 4.0 * ((offset + jnp.arange(energies_here)).astype(jnp.float32) + 0.5) / total
    identity = jnp.eye(order, dtype=jnp.float32)
    shift = sigma_shift[:, 0]
    width = sigma_width[:, 0]
    source = 2.0 * occupation[:, 0] * width
    real_part = (
        energy[:, None, None] * identity
        - ham_diag[None, 0, 0]
        - shift[:, :, None] * identity
    )
    imag_part = width[:, :, None] * identity - ham_diag[None, 0, 1]
    system = embed(real_part, imag_part)

    green_col = invert(system)
    g_re, g_im = split(green_col)
    scaled = embed(-g_im * source[:, None, :], g_re * source[:, None, :])
    far_green = from_partner(green_col, "space", 0)
    green_less = dot(scaled, stacked_adjoint(g_re, g_im), lax.Precision.HIGH)
    far_less = from_partner(green_less, "space", 0)

    link = ham_coupling[0]
    link_re = jnp.where(first, link[0], swap(link[0]))
    link_im = jnp.where(first, link[1], -swap(link[1]))
    link_embed = lax.optimization_barrier(embed(link_re, link_im))
    link_adj = stacked_adjoint(link_re, link_im)
    high = lax.Precision.HIGH
    left_green = dot(link_embed, far_green, high)
    coupled_green = dot(embed(*split(left_green)), link_adj, high)
    left_less = dot(link_embed, far_less, high)
    coupled_less = dot(embed(*split(left_less)), link_adj, high)

    full_re, full_im = split(invert(system - embed(*split(coupled_green))))
    less_re, less_im = split(coupled_less)
    less_im = less_im + source[:, :, None] * identity
    inner = dot(embed(full_re, full_im), stack(less_re, less_im))
    lesser = dot(embed(*split(inner)), stacked_adjoint(full_re, full_im))
    lesser_re, lesser_im = split(lesser)
    greater_re = lesser_re + full_re - swap(full_re)
    greater_im = lesser_im + full_im + swap(full_im)

    chunks = lax.axis_size("energy") * lax.axis_size("space")
    row_count = order // chunks
    parts = [lesser_re, lesser_im, greater_re, greater_im]
    parts = [part.reshape((energies_here, chunks, row_count, order)) for part in parts]
    paired = jnp.moveaxis(jnp.stack(parts, axis=2), 1, 0)
    arrived = lax.all_to_all(paired, ("energy", "space"), split_axis=0, concat_axis=0, tiled=True)
    arrived = arrived.reshape(
        (lax.axis_size("energy"), lax.axis_size("space"), energies_here, 4, row_count, order)
    )
    arrived = jnp.transpose(arrived, (0, 2, 1, 3, 4, 5))
    regrouped = arrived.reshape((total, lax.axis_size("space"), 2, 2, row_count, order))
    a_re, a_im = regrouped[:, :, 0, 0], regrouped[:, :, 0, 1]
    b_re, b_im = regrouped[:, :, 1, 0], regrouped[:, :, 1, 1]
    corr_re = []
    corr_im = []
    for shift_index in range(total):
        upper_re, upper_im = a_re[shift_index:], a_im[shift_index:]
        lower_re, lower_im = b_re[: total - shift_index], b_im[: total - shift_index]
        corr_re.append(jnp.sum(upper_re * lower_re + upper_im * lower_im, axis=0))
        corr_im.append(jnp.sum(upper_im * lower_re - upper_re * lower_im, axis=0))
    corr_re = jnp.stack(corr_re, axis=0)
    corr_im = jnp.stack(corr_im, axis=0)
    return jnp.stack([-order * corr_im, order * corr_re], axis=2)


def solution(mesh):
    return jax.shard_map(
        body,
        mesh=mesh,
        in_specs=(
            P("space", None, "groups", None),
            P("groups", None, None, None),
            P("energy", "space", "groups"),
            P("energy", "space", "groups"),
            P("energy", "space", "groups"),
        ),
        out_specs=P("groups", None, None, ("energy", "space"), None),
        check_vma=False,
    )
```

```python
import jax
import jax.numpy as jnp
from jax import lax
from jax.sharding import PartitionSpec as P


def from_partner(shard, axis, distance):
    return lax.ppermute(shard, axis, [(i, i ^ 1 << distance) for i in range(lax.axis_size(axis))])


def dot(left, right, precision=lax.Precision.HIGHEST):
    return jnp.einsum("...ij,...jk->...ik", left, right, precision=precision)


def swap(value):
    return jnp.swapaxes(value, -1, -2)


def embed(real, imag):
    top = jnp.concatenate([real, -imag], axis=-1)
    bottom = jnp.concatenate([imag, real], axis=-1)
    return jnp.concatenate([top, bottom], axis=-2)


def stack(real, imag):
    return jnp.concatenate([real, imag], axis=-2)


def split(stacked):
    order = stacked.shape[-2] // 2
    return stacked[..., :order, :], stacked[..., order:, :]


def stacked_adjoint(real, imag):
    return stack(swap(real), -swap(imag))


def invert(matrix):
    order = matrix.shape[-1] // 2
    eye = stack(jnp.eye(order, dtype=jnp.float32), jnp.zeros((order, order), jnp.float32))
    high = lax.Precision.HIGH
    gram = jnp.einsum("...ij,...kj->...ik", matrix, matrix[..., :order, :], precision=high)
    square = dot(embed(*split(gram)), gram, high)
    square_re, square_im = split(square)
    rows = jnp.sum(jnp.abs(square_re) + jnp.abs(square_im), axis=-1)
    beta = jnp.sqrt(jnp.max(rows, axis=-1)) * 1.01 + 1e-30
    beta = beta[..., None, None]
    lower = 0.25 / beta
    alpha = 2.0 / (lower + 1.0)
    first_step = 2.0 * eye - (alpha / beta) * gram
    approx = jnp.einsum("...ji,...jk->...ik", matrix, first_step, precision=high) * (alpha / beta)
    ratio = (1.0 - lower) / (1.0 + lower)
    lower = 1.0 - ratio * ratio
    for _ in range(6):
        alpha = 2.0 / (lower + 1.0)
        product = dot(matrix, approx, high)
        approx = dot(alpha * embed(*split(approx)), 2.0 * eye - alpha * product, high)
        ratio = (1.0 - lower) / (1.0 + lower)
        lower = 1.0 - ratio * ratio

    def keep_going(state):
        _, residual, count = state
        return (residual > 7e-4) & (count < 40)

    def newton(state):
        approx, _, count = state
        rest = eye - dot(matrix, approx)
        residual = jnp.sqrt(jnp.max(jnp.sum(rest * rest, axis=(-1, -2))))
        return approx + dot(embed(*split(approx)), rest, high), residual, count + 1

    approx, _, _ = lax.while_loop(
        keep_going, newton, (approx, jnp.float32(jnp.inf), jnp.int32(0))
    )
    return approx


def body(ham_diag, ham_coupling, sigma_shift, sigma_width, occupation):
    blocks = ham_diag.shape[0]
    assert blocks == 1
    energies_here = sigma_shift.shape[0]
    order = ham_diag.shape[-1]
    side = lax.axis_index("space")
    first = side == 0
    total = energies_here * lax.axis_size("energy")
    offset = lax.axis_index("energy") * energies_here
    energy = -2.0 + 4.0 * ((offset + jnp.arange(energies_here)).astype(jnp.float32) + 0.5) / total
    identity = jnp.eye(order, dtype=jnp.float32)
    shift = sigma_shift[:, 0]
    width = sigma_width[:, 0]
    source = 2.0 * occupation[:, 0] * width
    real_part = (
        energy[:, None, None] * identity
        - ham_diag[None, 0, 0]
        - shift[:, :, None] * identity
    )
    imag_part = width[:, :, None] * identity - ham_diag[None, 0, 1]
    system = embed(real_part, imag_part)

    green_col = invert(system)
    g_re, g_im = split(green_col)
    scaled = embed(-g_im * source[:, None, :], g_re * source[:, None, :])
    link = ham_coupling[0]
    link_re = jnp.where(first, swap(link[0]), link[0])
    link_im = jnp.where(first, -swap(link[1]), link[1])
    link_embed = embed(link_re, link_im)
    link_adj = stacked_adjoint(link_re, link_im)
    high = lax.Precision.HIGH
    left_green = dot(link_embed, green_col, high)
    coupled_green = from_partner(dot(embed(*split(left_green)), link_adj, high), "space", 0)
    green_less = dot(scaled, stacked_adjoint(g_re, g_im))
    left_less = dot(link_embed, green_less, high)
    coupled_less = from_partner(dot(embed(*split(left_less)), link_adj, high), "space", 0)

    full_re, full_im = split(invert(system - embed(*split(coupled_green))))
    less_re, less_im = split(coupled_less)
    less_im = less_im + source[:, :, None] * identity
    inner = dot(embed(full_re, full_im), stack(less_re, less_im))
    lesser = dot(embed(*split(inner)), stacked_adjoint(full_re, full_im))
    lesser_re, lesser_im = split(lesser)
    greater_re = lesser_re + full_re - swap(full_re)
    greater_im = lesser_im + full_im + swap(full_im)

    chunks = lax.axis_size("energy") * lax.axis_size("space")
    row_count = order // chunks
    parts = [lesser_re, lesser_im, greater_re, greater_im]
    parts = [part.reshape((energies_here, chunks, row_count, order)) for part in parts]
    paired = jnp.moveaxis(jnp.stack(parts, axis=2), 1, 0)
    arrived = lax.all_to_all(paired, ("energy", "space"), split_axis=0, concat_axis=0, tiled=True)
    arrived = arrived.reshape(
        (lax.axis_size("energy"), lax.axis_size("space"), energies_here, 4, row_count, order)
    )
    arrived = jnp.transpose(arrived, (0, 2, 1, 3, 4, 5))
    regrouped = arrived.reshape((total, lax.axis_size("space"), 2, 2, row_count, order))
    a_re, a_im = regrouped[:, :, 0, 0], regrouped[:, :, 0, 1]
    b_re, b_im = regrouped[:, :, 1, 0], regrouped[:, :, 1, 1]
    corr_re = []
    corr_im = []
    for shift_index in range(total):
        upper_re, upper_im = a_re[shift_index:], a_im[shift_index:]
        lower_re, lower_im = b_re[: total - shift_index], b_im[: total - shift_index]
        corr_re.append(jnp.sum(upper_re * lower_re + upper_im * lower_im, axis=0))
        corr_im.append(jnp.sum(upper_im * lower_re - upper_re * lower_im, axis=0))
    corr_re = jnp.stack(corr_re, axis=0)
    corr_im = jnp.stack(corr_im, axis=0)
    return jnp.stack([-order * corr_im, order * corr_re], axis=2)


def solution(mesh):
    return jax.shard_map(
        body,
        mesh=mesh,
        in_specs=(
            P("space", None, "groups", None),
            P("groups", None, None, None),
            P("energy", "space", "groups"),
            P("energy", "space", "groups"),
            P("energy", "space", "groups"),
        ),
        out_specs=P("groups", None, None, ("energy", "space"), None),
        check_vma=False,
    )
```

```python
import jax
import jax.numpy as jnp
from jax import lax
from jax.sharding import PartitionSpec as P


def from_partner(shard, axis, distance):
    return lax.ppermute(shard, axis, [(i, i ^ 1 << distance) for i in range(lax.axis_size(axis))])


def dot(left, right, precision=lax.Precision.HIGHEST):
    return jnp.einsum("...ij,...jk->...ik", left, right, precision=precision)


def swap(value):
    return jnp.swapaxes(value, -1, -2)


def embed(real, imag):
    top = jnp.concatenate([real, -imag], axis=-1)
    bottom = jnp.concatenate([imag, real], axis=-1)
    return jnp.concatenate([top, bottom], axis=-2)


def stack(real, imag):
    return jnp.concatenate([real, imag], axis=-2)


def split(stacked):
    order = stacked.shape[-2] // 2
    return stacked[..., :order, :], stacked[..., order:, :]


def stacked_adjoint(real, imag):
    return stack(swap(real), -swap(imag))


def invert(matrix):
    order = matrix.shape[-1] // 2
    eye = stack(jnp.eye(order, dtype=jnp.float32), jnp.zeros((order, order), jnp.float32))
    high = lax.Precision.HIGH
    gram = jnp.einsum("...ij,...kj->...ik", matrix, matrix[..., :order, :], precision=high)
    square = dot(embed(*split(gram)), gram, high)
    fourth = dot(embed(*split(square)), square, high)
    fourth_re, fourth_im = split(fourth)
    rows = jnp.sum(jnp.abs(fourth_re) + jnp.abs(fourth_im), axis=-1)
    beta = jnp.sqrt(jnp.sqrt(jnp.max(rows, axis=-1))) * 1.01 + 1e-30
    beta = beta[..., None, None]
    lower = 0.25 / beta
    alpha = 2.0 / (lower + 1.0)
    first_step = 2.0 * eye - (alpha / beta) * gram
    approx = jnp.einsum("...ji,...jk->...ik", matrix, first_step, precision=high) * (alpha / beta)
    ratio = (1.0 - lower) / (1.0 + lower)
    lower = 1.0 - ratio * ratio
    for _ in range(5):
        alpha = 2.0 / (lower + 1.0)
        product = dot(matrix, approx, high)
        approx = dot(alpha * embed(*split(approx)), 2.0 * eye - alpha * product, high)
        ratio = (1.0 - lower) / (1.0 + lower)
        lower = 1.0 - ratio * ratio

    def keep_going(state):
        _, residual, count = state
        return (residual > 2e-3) & (count < 40)

    def newton(state):
        approx, _, count = state
        rest = eye - dot(matrix, approx)
        residual = jnp.sqrt(jnp.max(jnp.sum(rest * rest, axis=(-1, -2))))
        return approx + dot(embed(*split(approx)), rest, high), residual, count + 1

    approx, _, _ = lax.while_loop(
        keep_going, newton, (approx, jnp.float32(jnp.inf), jnp.int32(0))
    )
    return approx


def body(ham_diag, ham_coupling, sigma_shift, sigma_width, occupation):
    blocks = ham_diag.shape[0]
    assert blocks == 1
    energies_here = sigma_shift.shape[0]
    order = ham_diag.shape[-1]
    side = lax.axis_index("space")
    first = side == 0
    total = energies_here * lax.axis_size("energy")
    offset = lax.axis_index("energy") * energies_here
    energy = -2.0 + 4.0 * ((offset + jnp.arange(energies_here)).astype(jnp.float32) + 0.5) / total
    identity = jnp.eye(order, dtype=jnp.float32)
    shift = sigma_shift[:, 0]
    width = sigma_width[:, 0]
    source = 2.0 * occupation[:, 0] * width
    real_part = (
        energy[:, None, None] * identity
        - ham_diag[None, 0, 0]
        - shift[:, :, None] * identity
    )
    imag_part = width[:, :, None] * identity - ham_diag[None, 0, 1]
    system = embed(real_part, imag_part)

    green_col = invert(system)
    g_re, g_im = split(green_col)
    scaled = embed(-g_im * source[:, None, :], g_re * source[:, None, :])
    link = ham_coupling[0]
    link_re = jnp.where(first, swap(link[0]), link[0])
    link_im = jnp.where(first, -swap(link[1]), link[1])
    link_embed = embed(link_re, link_im)
    link_adj = stacked_adjoint(link_re, link_im)
    high = lax.Precision.HIGH
    left_green = dot(link_embed, green_col, high)
    coupled_green = from_partner(dot(embed(*split(left_green)), link_adj, high), "space", 0)
    green_less = dot(scaled, stacked_adjoint(g_re, g_im), high)
    left_less = dot(link_embed, green_less, high)
    coupled_less = from_partner(dot(embed(*split(left_less)), link_adj, high), "space", 0)

    full_re, full_im = split(invert(system - embed(*split(coupled_green))))
    less_re, less_im = split(coupled_less)
    less_im = less_im + source[:, :, None] * identity
    inner = dot(embed(full_re, full_im), stack(less_re, less_im))
    lesser = dot(embed(*split(inner)), stacked_adjoint(full_re, full_im))
    lesser_re, lesser_im = split(lesser)
    greater_re = lesser_re + full_re - swap(full_re)
    greater_im = lesser_im + full_im + swap(full_im)

    chunks = lax.axis_size("energy") * lax.axis_size("space")
    row_count = order // chunks
    parts = [lesser_re, lesser_im, greater_re, greater_im]
    parts = [part.reshape((energies_here, chunks, row_count, order)) for part in parts]
    paired = jnp.moveaxis(jnp.stack(parts, axis=2), 1, 0)
    arrived = lax.all_to_all(paired, ("energy", "space"), split_axis=0, concat_axis=0, tiled=True)
    arrived = arrived.reshape(
        (lax.axis_size("energy"), lax.axis_size("space"), energies_here, 4, row_count, order)
    )
    arrived = jnp.transpose(arrived, (0, 2, 1, 3, 4, 5))
    regrouped = arrived.reshape((total, lax.axis_size("space"), 2, 2, row_count, order))
    a_re, a_im = regrouped[:, :, 0, 0], regrouped[:, :, 0, 1]
    b_re, b_im = regrouped[:, :, 1, 0], regrouped[:, :, 1, 1]
    corr_re = []
    corr_im = []
    for shift_index in range(total):
        upper_re, upper_im = a_re[shift_index:], a_im[shift_index:]
        lower_re, lower_im = b_re[: total - shift_index], b_im[: total - shift_index]
        corr_re.append(jnp.sum(upper_re * lower_re + upper_im * lower_im, axis=0))
        corr_im.append(jnp.sum(upper_im * lower_re - upper_re * lower_im, axis=0))
    corr_re = jnp.stack(corr_re, axis=0)
    corr_im = jnp.stack(corr_im, axis=0)
    return jnp.stack([-order * corr_im, order * corr_re], axis=2)


def solution(mesh):
    return jax.shard_map(
        body,
        mesh=mesh,
        in_specs=(
            P("space", None, "groups", None),
            P("groups", None, None, None),
            P("energy", "space", "groups"),
            P("energy", "space", "groups"),
            P("energy", "space", "groups"),
        ),
        out_specs=P("groups", None, None, ("energy", "space"), None),
        check_vma=False,
    )
```

```python
import jax
import jax.numpy as jnp
from jax import lax
from jax.sharding import PartitionSpec as P


def from_partner(shard, axis, distance):
    return lax.ppermute(shard, axis, [(i, i ^ 1 << distance) for i in range(lax.axis_size(axis))])


def dot(left, right, precision=lax.Precision.HIGHEST):
    return jnp.einsum("...ij,...jk->...ik", left, right, precision=precision)


def swap(value):
    return jnp.swapaxes(value, -1, -2)


def embed(real, imag):
    top = jnp.concatenate([real, -imag], axis=-1)
    bottom = jnp.concatenate([imag, real], axis=-1)
    return jnp.concatenate([top, bottom], axis=-2)


def stack(real, imag):
    return jnp.concatenate([real, imag], axis=-2)


def split(stacked):
    order = stacked.shape[-2] // 2
    return stacked[..., :order, :], stacked[..., order:, :]


def stacked_adjoint(real, imag):
    return stack(swap(real), -swap(imag))


def invert(matrix):
    order = matrix.shape[-1] // 2
    eye = stack(jnp.eye(order, dtype=jnp.float32), jnp.zeros((order, order), jnp.float32))
    high = lax.Precision.HIGH
    gram = jnp.einsum("...ij,...kj->...ik", matrix, matrix[..., :order, :], precision=high)
    square = dot(embed(*split(gram)), gram, high)
    fourth = dot(embed(*split(square)), square, high)
    fourth_re, fourth_im = split(fourth)
    rows = jnp.sum(jnp.abs(fourth_re) + jnp.abs(fourth_im), axis=-1)
    beta = jnp.sqrt(jnp.sqrt(jnp.max(rows, axis=-1))) * 1.01 + 1e-30
    beta = beta[..., None, None]
    lower = 0.25 / beta
    alpha = 2.0 / (lower + 1.0)
    first_step = 2.0 * eye - (alpha / beta) * gram
    approx = jnp.einsum("...ji,...jk->...ik", matrix, first_step, precision=high) * (alpha / beta)
    ratio = (1.0 - lower) / (1.0 + lower)
    lower = 1.0 - ratio * ratio
    for _ in range(5):
        alpha = 2.0 / (lower + 1.0)
        product = dot(matrix, approx, high)
        approx = dot(alpha * embed(*split(approx)), 2.0 * eye - alpha * product, high)
        ratio = (1.0 - lower) / (1.0 + lower)
        lower = 1.0 - ratio * ratio

    def keep_going(state):
        _, residual, count = state
        return (residual > 2e-3) & (count < 40)

    def newton(state):
        approx, _, count = state
        rest = eye - dot(matrix, approx)
        residual = jnp.sqrt(jnp.max(jnp.sum(rest * rest, axis=(-1, -2))))
        return approx + dot(embed(*split(approx)), rest, high), residual, count + 1

    approx, _, _ = lax.while_loop(
        keep_going, newton, (approx, jnp.float32(jnp.inf), jnp.int32(0))
    )
    return approx


def body(ham_diag, ham_coupling, sigma_shift, sigma_width, occupation):
    blocks = ham_diag.shape[0]
    assert blocks == 1
    energies_here = sigma_shift.shape[0]
    order = ham_diag.shape[-1]
    side = lax.axis_index("space")
    first = side == 0
    total = energies_here * lax.axis_size("energy")
    offset = lax.axis_index("energy") * energies_here
    energy = -2.0 + 4.0 * ((offset + jnp.arange(energies_here)).astype(jnp.float32) + 0.5) / total
    identity = jnp.eye(order, dtype=jnp.float32)
    shift = sigma_shift[:, 0]
    width = sigma_width[:, 0]
    source = 2.0 * occupation[:, 0] * width
    real_part = (
        energy[:, None, None] * identity
        - ham_diag[None, 0, 0]
        - shift[:, :, None] * identity
    )
    imag_part = width[:, :, None] * identity - ham_diag[None, 0, 1]
    system = embed(real_part, imag_part)

    green_col = invert(system)
    g_re, g_im = split(green_col)
    scaled = embed(-g_im * source[:, None, :], g_re * source[:, None, :])
    link = ham_coupling[0]
    link_re = jnp.where(first, swap(link[0]), link[0])
    link_im = jnp.where(first, -swap(link[1]), link[1])
    link_embed = embed(link_re, link_im)
    link_adj = stacked_adjoint(link_re, link_im)
    high = lax.Precision.HIGH
    left_green = dot(link_embed, green_col, high)
    coupled_green = from_partner(dot(embed(*split(left_green)), link_adj, high), "space", 0)
    green_less = dot(scaled, stacked_adjoint(g_re, g_im), high)
    left_less = dot(link_embed, green_less, high)
    coupled_less = from_partner(dot(embed(*split(left_less)), link_adj, high), "space", 0)

    full_re, full_im = split(invert(system - embed(*split(coupled_green))))
    less_re, less_im = split(coupled_less)
    less_im = less_im + source[:, :, None] * identity
    inner = dot(embed(full_re, full_im), stack(less_re, less_im), high)
    lesser = dot(embed(*split(inner)), stacked_adjoint(full_re, full_im), high)
    lesser_re, lesser_im = split(lesser)
    greater_re = lesser_re + full_re - swap(full_re)
    greater_im = lesser_im + full_im + swap(full_im)

    chunks = lax.axis_size("energy") * lax.axis_size("space")
    row_count = order // chunks
    parts = [lesser_re, lesser_im, greater_re, greater_im]
    parts = [part.reshape((energies_here, chunks, row_count, order)) for part in parts]
    paired = jnp.moveaxis(jnp.stack(parts, axis=2), 1, 0)
    arrived = lax.all_to_all(paired, ("energy", "space"), split_axis=0, concat_axis=0, tiled=True)
    arrived = arrived.reshape(
        (lax.axis_size("energy"), lax.axis_size("space"), energies_here, 4, row_count, order)
    )
    arrived = jnp.transpose(arrived, (0, 2, 1, 3, 4, 5))
    regrouped = arrived.reshape((total, lax.axis_size("space"), 2, 2, row_count, order))
    a_re, a_im = regrouped[:, :, 0, 0], regrouped[:, :, 0, 1]
    b_re, b_im = regrouped[:, :, 1, 0], regrouped[:, :, 1, 1]
    corr_re = []
    corr_im = []
    for shift_index in range(total):
        upper_re, upper_im = a_re[shift_index:], a_im[shift_index:]
        lower_re, lower_im = b_re[: total - shift_index], b_im[: total - shift_index]
        corr_re.append(jnp.sum(upper_re * lower_re + upper_im * lower_im, axis=0))
        corr_im.append(jnp.sum(upper_im * lower_re - upper_re * lower_im, axis=0))
    corr_re = jnp.stack(corr_re, axis=0)
    corr_im = jnp.stack(corr_im, axis=0)
    return jnp.stack([-order * corr_im, order * corr_re], axis=2)


def solution(mesh):
    return jax.shard_map(
        body,
        mesh=mesh,
        in_specs=(
            P("space", None, "groups", None),
            P("groups", None, None, None),
            P("energy", "space", "groups"),
            P("energy", "space", "groups"),
            P("energy", "space", "groups"),
        ),
        out_specs=P("groups", None, None, ("energy", "space"), None),
        check_vma=False,
    )
```

```python
import jax
import jax.numpy as jnp
from jax import lax
from jax.sharding import PartitionSpec as P


def from_partner(shard, axis, distance):
    return lax.ppermute(shard, axis, [(i, i ^ 1 << distance) for i in range(lax.axis_size(axis))])


def dot(left, right, precision=lax.Precision.HIGHEST):
    return jnp.einsum("...ij,...jk->...ik", left, right, precision=precision)


def swap(value):
    return jnp.swapaxes(value, -1, -2)


def embed(real, imag):
    top = jnp.concatenate([real, -imag], axis=-1)
    bottom = jnp.concatenate([imag, real], axis=-1)
    return jnp.concatenate([top, bottom], axis=-2)


def stack(real, imag):
    return jnp.concatenate([real, imag], axis=-2)


def split(stacked):
    order = stacked.shape[-2] // 2
    return stacked[..., :order, :], stacked[..., order:, :]


def stacked_adjoint(real, imag):
    return stack(swap(real), -swap(imag))


def invert(matrix):
    order = matrix.shape[-1] // 2
    eye = stack(jnp.eye(order, dtype=jnp.float32), jnp.zeros((order, order), jnp.float32))
    high = lax.Precision.HIGH
    gram = jnp.einsum("...ij,...kj->...ik", matrix, matrix[..., :order, :], precision=high)
    square = dot(embed(*split(gram)), gram, high)
    fourth = dot(embed(*split(square)), square, high)
    fourth_re, fourth_im = split(fourth)
    rows = jnp.sum(jnp.abs(fourth_re) + jnp.abs(fourth_im), axis=-1)
    beta = jnp.sqrt(jnp.sqrt(jnp.max(rows, axis=-1))) * 1.01 + 1e-30
    beta = beta[..., None, None]
    lower = 0.25 / beta
    alpha = 2.0 / (lower + 1.0)
    first_step = 2.0 * eye - (alpha / beta) * gram
    approx = jnp.einsum("...ji,...jk->...ik", matrix, first_step, precision=high) * (alpha / beta)
    ratio = (1.0 - lower) / (1.0 + lower)
    lower = 1.0 - ratio * ratio
    for _ in range(5):
        alpha = 2.0 / (lower + 1.0)
        product = dot(matrix, approx, high)
        approx = dot(alpha * embed(*split(approx)), 2.0 * eye - alpha * product, high)
        ratio = (1.0 - lower) / (1.0 + lower)
        lower = 1.0 - ratio * ratio

    def keep_going(state):
        _, residual, count = state
        return (residual > 2e-3) & (count < 40)

    def newton(state):
        approx, _, count = state
        rest = eye - dot(matrix, approx)
        residual = jnp.sqrt(jnp.max(jnp.sum(rest * rest, axis=(-1, -2))))
        return approx + dot(embed(*split(approx)), rest, high), residual, count + 1

    state = newton((approx, None, jnp.int32(0)))
    approx, _, _ = lax.while_loop(keep_going, newton, state)
    return approx


def body(ham_diag, ham_coupling, sigma_shift, sigma_width, occupation):
    blocks = ham_diag.shape[0]
    assert blocks == 1
    energies_here = sigma_shift.shape[0]
    order = ham_diag.shape[-1]
    side = lax.axis_index("space")
    first = side == 0
    total = energies_here * lax.axis_size("energy")
    offset = lax.axis_index("energy") * energies_here
    energy = -2.0 + 4.0 * ((offset + jnp.arange(energies_here)).astype(jnp.float32) + 0.5) / total
    identity = jnp.eye(order, dtype=jnp.float32)
    shift = sigma_shift[:, 0]
    width = sigma_width[:, 0]
    source = 2.0 * occupation[:, 0] * width
    real_part = (
        energy[:, None, None] * identity
        - ham_diag[None, 0, 0]
        - shift[:, :, None] * identity
    )
    imag_part = width[:, :, None] * identity - ham_diag[None, 0, 1]
    system = embed(real_part, imag_part)

    green_col = invert(system)
    g_re, g_im = split(green_col)
    scaled = embed(-g_im * source[:, None, :], g_re * source[:, None, :])
    link = ham_coupling[0]
    link_re = jnp.where(first, swap(link[0]), link[0])
    link_im = jnp.where(first, -swap(link[1]), link[1])
    link_embed = embed(link_re, link_im)
    link_adj = stacked_adjoint(link_re, link_im)
    high = lax.Precision.HIGH
    left_green = dot(link_embed, green_col, high)
    coupled_green = from_partner(dot(embed(*split(left_green)), link_adj, high), "space", 0)
    green_less = dot(scaled, stacked_adjoint(g_re, g_im), high)
    left_less = dot(link_embed, green_less, high)
    coupled_less = from_partner(dot(embed(*split(left_less)), link_adj, high), "space", 0)

    full_re, full_im = split(invert(system - embed(*split(coupled_green))))
    less_re, less_im = split(coupled_less)
    less_im = less_im + source[:, :, None] * identity
    inner = dot(embed(full_re, full_im), stack(less_re, less_im), high)
    lesser = dot(embed(*split(inner)), stacked_adjoint(full_re, full_im), high)
    lesser_re, lesser_im = split(lesser)
    greater_re = lesser_re + full_re - swap(full_re)
    greater_im = lesser_im + full_im + swap(full_im)

    chunks = lax.axis_size("energy") * lax.axis_size("space")
    row_count = order // chunks
    parts = [lesser_re, lesser_im, greater_re, greater_im]
    parts = [part.reshape((energies_here, chunks, row_count, order)) for part in parts]
    paired = jnp.moveaxis(jnp.stack(parts, axis=2), 1, 0)
    arrived = lax.all_to_all(paired, ("energy", "space"), split_axis=0, concat_axis=0, tiled=True)
    arrived = arrived.reshape(
        (lax.axis_size("energy"), lax.axis_size("space"), energies_here, 4, row_count, order)
    )
    arrived = jnp.transpose(arrived, (0, 2, 1, 3, 4, 5))
    regrouped = arrived.reshape((total, lax.axis_size("space"), 2, 2, row_count, order))
    a_re, a_im = regrouped[:, :, 0, 0], regrouped[:, :, 0, 1]
    b_re, b_im = regrouped[:, :, 1, 0], regrouped[:, :, 1, 1]
    corr_re = []
    corr_im = []
    for shift_index in range(total):
        upper_re, upper_im = a_re[shift_index:], a_im[shift_index:]
        lower_re, lower_im = b_re[: total - shift_index], b_im[: total - shift_index]
        corr_re.append(jnp.sum(upper_re * lower_re + upper_im * lower_im, axis=0))
        corr_im.append(jnp.sum(upper_im * lower_re - upper_re * lower_im, axis=0))
    corr_re = jnp.stack(corr_re, axis=0)
    corr_im = jnp.stack(corr_im, axis=0)
    return jnp.stack([-order * corr_im, order * corr_re], axis=2)


def solution(mesh):
    return jax.shard_map(
        body,
        mesh=mesh,
        in_specs=(
            P("space", None, "groups", None),
            P("groups", None, None, None),
            P("energy", "space", "groups"),
            P("energy", "space", "groups"),
            P("energy", "space", "groups"),
        ),
        out_specs=P("groups", None, None, ("energy", "space"), None),
        check_vma=False,
    )
```

```python
import jax
import jax.numpy as jnp
from jax import lax
from jax.sharding import PartitionSpec as P


def from_partner(shard, axis, distance):
    return lax.ppermute(shard, axis, [(i, i ^ 1 << distance) for i in range(lax.axis_size(axis))])


def dot(left, right, precision=lax.Precision.HIGHEST):
    return jnp.einsum("...ij,...jk->...ik", left, right, precision=precision)


def swap(value):
    return jnp.swapaxes(value, -1, -2)


def embed(real, imag):
    top = jnp.concatenate([real, -imag], axis=-1)
    bottom = jnp.concatenate([imag, real], axis=-1)
    return jnp.concatenate([top, bottom], axis=-2)


def stack(real, imag):
    return jnp.concatenate([real, imag], axis=-2)


def split(stacked):
    order = stacked.shape[-2] // 2
    return stacked[..., :order, :], stacked[..., order:, :]


def stacked_adjoint(real, imag):
    return stack(swap(real), -swap(imag))


def invert(matrix):
    order = matrix.shape[-1] // 2
    eye = stack(jnp.eye(order, dtype=jnp.float32), jnp.zeros((order, order), jnp.float32))
    high = lax.Precision.HIGH
    gram = jnp.einsum("...ij,...kj->...ik", matrix, matrix[..., :order, :], precision=high)
    square = dot(embed(*split(gram)), gram, high)
    fourth = dot(embed(*split(square)), square, high)
    fourth_re, fourth_im = split(fourth)
    rows = jnp.sum(jnp.abs(fourth_re) + jnp.abs(fourth_im), axis=-1)
    beta = jnp.sqrt(jnp.sqrt(jnp.max(rows, axis=-1))) * 1.01 + 1e-30
    beta = beta[..., None, None]
    lower = 0.25 / beta
    alpha = 2.0 / (lower + 1.0)
    first_step = 2.0 * eye - (alpha / beta) * gram
    approx = jnp.einsum("...ji,...jk->...ik", matrix, first_step, precision=high) * (alpha / beta)
    ratio = (1.0 - lower) / (1.0 + lower)
    lower = 1.0 - ratio * ratio
    for _ in range(5):
        alpha = 2.0 / (lower + 1.0)
        product = dot(matrix, approx, high)
        approx = dot(alpha * embed(*split(approx)), 2.0 * eye - alpha * product, high)
        ratio = (1.0 - lower) / (1.0 + lower)
        lower = 1.0 - ratio * ratio

    def keep_going(state):
        _, residual, count = state
        return (residual > 2e-3) & (count < 40)

    def newton(state):
        approx, _, count = state
        rest = eye - dot(matrix, approx)
        residual = jnp.sqrt(jnp.max(jnp.sum(rest * rest, axis=(-1, -2))))
        return approx + dot(embed(*split(approx)), rest, high), residual, count + 1

    approx, _, _ = lax.while_loop(
        keep_going, newton, (approx, jnp.float32(jnp.inf), jnp.int32(0))
    )
    return approx


def body(ham_diag, ham_coupling, sigma_shift, sigma_width, occupation):
    blocks = ham_diag.shape[0]
    assert blocks == 1
    energies_here = sigma_shift.shape[0]
    order = ham_diag.shape[-1]
    side = lax.axis_index("space")
    first = side == 0
    total = energies_here * lax.axis_size("energy")
    offset = lax.axis_index("energy") * energies_here
    energy = -2.0 + 4.0 * ((offset + jnp.arange(energies_here)).astype(jnp.float32) + 0.5) / total
    identity = jnp.eye(order, dtype=jnp.float32)
    shift = sigma_shift[:, 0]
    width = sigma_width[:, 0]
    source = 2.0 * occupation[:, 0] * width
    real_part = (
        energy[:, None, None] * identity
        - ham_diag[None, 0, 0]
        - shift[:, :, None] * identity
    )
    imag_part = width[:, :, None] * identity - ham_diag[None, 0, 1]
    system = embed(real_part, imag_part)

    green_col = invert(system)
    g_re, g_im = split(green_col)
    scaled = embed(-g_im * source[:, None, :], g_re * source[:, None, :])
    link = ham_coupling[0]
    link_re = jnp.where(first, swap(link[0]), link[0])
    link_im = jnp.where(first, -swap(link[1]), link[1])
    link_embed = embed(link_re, link_im)
    link_adj = stacked_adjoint(link_re, link_im)
    high = lax.Precision.HIGH
    left_green = dot(link_embed, green_col, high)
    coupled_green = from_partner(dot(embed(*split(left_green)), link_adj, high), "space", 0)
    green_less = dot(scaled, stacked_adjoint(g_re, g_im), high)
    left_less = dot(link_embed, green_less, high)
    coupled_less = from_partner(dot(embed(*split(left_less)), link_adj, high), "space", 0)

    full_re, full_im = split(invert(system - embed(*split(coupled_green))))
    less_re, less_im = split(coupled_less)
    less_im = less_im + source[:, :, None] * identity
    inner = dot(embed(full_re, full_im), stack(less_re, less_im), high)
    lesser = dot(embed(*split(inner)), stacked_adjoint(full_re, full_im), high)
    lesser_re, lesser_im = split(lesser)
    greater_re = lesser_re + full_re - swap(full_re)
    greater_im = lesser_im + full_im + swap(full_im)

    chunks = lax.axis_size("energy") * lax.axis_size("space")
    row_count = order // chunks
    parts = [lesser_re, lesser_im, greater_re, greater_im]
    parts = [part.reshape((energies_here, chunks, row_count, order)) for part in parts]
    paired = jnp.moveaxis(jnp.stack(parts, axis=2), 1, 0)
    arrived = lax.all_to_all(paired, ("energy", "space"), split_axis=0, concat_axis=0, tiled=True)
    arrived = arrived.reshape(
        (lax.axis_size("energy"), lax.axis_size("space"), energies_here, 4, row_count, order)
    )
    arrived = jnp.transpose(arrived, (0, 2, 1, 3, 4, 5))
    regrouped = arrived.reshape((total, lax.axis_size("space"), 2, 2, row_count, order))
    a_re, a_im = regrouped[:, :, 0, 0], regrouped[:, :, 0, 1]
    b_re, b_im = regrouped[:, :, 1, 0], regrouped[:, :, 1, 1]
    pad = jnp.zeros((total - 1,) + b_re.shape[1:], jnp.float32)
    padded_re = jnp.concatenate([pad, b_re], axis=0)
    padded_im = jnp.concatenate([pad, b_im], axis=0)
    lower_re = jnp.stack([padded_re[total - 1 - k : 2 * total - 1 - k] for k in range(total)])
    lower_im = jnp.stack([padded_im[total - 1 - k : 2 * total - 1 - k] for k in range(total)])
    corr_re = jnp.sum(a_re[None] * lower_re + a_im[None] * lower_im, axis=1)
    corr_im = jnp.sum(a_im[None] * lower_re - a_re[None] * lower_im, axis=1)
    return jnp.stack([-order * corr_im, order * corr_re], axis=2)


def solution(mesh):
    return jax.shard_map(
        body,
        mesh=mesh,
        in_specs=(
            P("space", None, "groups", None),
            P("groups", None, None, None),
            P("energy", "space", "groups"),
            P("energy", "space", "groups"),
            P("energy", "space", "groups"),
        ),
        out_specs=P("groups", None, None, ("energy", "space"), None),
        check_vma=False,
    )
```

```python
import jax
import jax.numpy as jnp
from jax import lax
from jax.sharding import PartitionSpec as P


def from_partner(shard, axis, distance):
    return lax.ppermute(shard, axis, [(i, i ^ 1 << distance) for i in range(lax.axis_size(axis))])


def dot(left, right, precision=lax.Precision.HIGHEST):
    return jnp.einsum("...ij,...jk->...ik", left, right, precision=precision)


def swap(value):
    return jnp.swapaxes(value, -1, -2)


def embed(real, imag):
    top = jnp.concatenate([real, -imag], axis=-1)
    bottom = jnp.concatenate([imag, real], axis=-1)
    return jnp.concatenate([top, bottom], axis=-2)


def stack(real, imag):
    return jnp.concatenate([real, imag], axis=-2)


def split(stacked):
    order = stacked.shape[-2] // 2
    return stacked[..., :order, :], stacked[..., order:, :]


def stacked_adjoint(real, imag):
    return stack(swap(real), -swap(imag))


def invert(matrix):
    order = matrix.shape[-1] // 2
    eye = stack(jnp.eye(order, dtype=jnp.float32), jnp.zeros((order, order), jnp.float32))
    high = lax.Precision.HIGH
    gram = jnp.einsum("...ij,...kj->...ik", matrix, matrix[..., :order, :], precision=high)
    square = dot(embed(*split(gram)), gram, high)
    fourth = dot(embed(*split(square)), square, high)
    fourth_re, fourth_im = split(fourth)
    rows = jnp.sum(jnp.abs(fourth_re) + jnp.abs(fourth_im), axis=-1)
    beta = jnp.sqrt(jnp.sqrt(jnp.max(rows, axis=-1))) * 1.01 + 1e-30
    beta = beta[..., None, None]
    lower = 0.25 / beta
    alpha = 2.0 / (lower + 1.0)
    first_step = 2.0 * eye - (alpha / beta) * gram
    approx = jnp.einsum("...ji,...jk->...ik", matrix, first_step, precision=high) * (alpha / beta)
    ratio = (1.0 - lower) / (1.0 + lower)
    lower = 1.0 - ratio * ratio
    for _ in range(5):
        alpha = 2.0 / (lower + 1.0)
        product = dot(matrix, approx, high)
        approx = dot(alpha * embed(*split(approx)), 2.0 * eye - alpha * product, high)
        ratio = (1.0 - lower) / (1.0 + lower)
        lower = 1.0 - ratio * ratio

    def keep_going(state):
        _, residual, count = state
        return (residual > 2e-3) & (count < 40)

    def newton(state):
        approx, _, count = state
        rest = eye - dot(matrix, approx)
        residual = jnp.sqrt(jnp.max(jnp.sum(rest * rest, axis=(-1, -2))))
        return approx + dot(embed(*split(approx)), rest, high), residual, count + 1

    approx, _, _ = lax.while_loop(
        keep_going, newton, (approx, jnp.float32(jnp.inf), jnp.int32(0))
    )
    return approx


def body(ham_diag, ham_coupling, sigma_shift, sigma_width, occupation):
    blocks = ham_diag.shape[0]
    assert blocks == 1
    energies_here = sigma_shift.shape[0]
    order = ham_diag.shape[-1]
    side = lax.axis_index("space")
    first = side == 0
    total = energies_here * lax.axis_size("energy")
    offset = lax.axis_index("energy") * energies_here
    energy = -2.0 + 4.0 * ((offset + jnp.arange(energies_here)).astype(jnp.float32) + 0.5) / total
    identity = jnp.eye(order, dtype=jnp.float32)
    shift = sigma_shift[:, 0]
    width = sigma_width[:, 0]
    source = 2.0 * occupation[:, 0] * width
    real_part = (
        energy[:, None, None] * identity
        - ham_diag[None, 0, 0]
        - shift[:, :, None] * identity
    )
    imag_part = width[:, :, None] * identity - ham_diag[None, 0, 1]
    system = embed(real_part, imag_part)

    green_col = invert(system)
    g_re, g_im = split(green_col)
    scaled = embed(-g_im * source[:, None, :], g_re * source[:, None, :])
    link = ham_coupling[0]
    def forms(real, imag):
        return embed(real, imag), stacked_adjoint(real, imag)

    link_embed, link_adj = lax.cond(
        first,
        lambda pair: forms(swap(pair[0]), -swap(pair[1])),
        lambda pair: forms(pair[0], pair[1]),
        link,
    )
    high = lax.Precision.HIGH
    left_green = dot(link_embed, green_col, high)
    coupled_green = from_partner(dot(embed(*split(left_green)), link_adj, high), "space", 0)
    green_less = dot(scaled, stacked_adjoint(g_re, g_im), high)
    left_less = dot(link_embed, green_less, high)
    coupled_less = from_partner(dot(embed(*split(left_less)), link_adj, high), "space", 0)

    full_re, full_im = split(invert(system - embed(*split(coupled_green))))
    less_re, less_im = split(coupled_less)
    less_im = less_im + source[:, :, None] * identity
    inner = dot(embed(full_re, full_im), stack(less_re, less_im), high)
    lesser = dot(embed(*split(inner)), stacked_adjoint(full_re, full_im), high)
    lesser_re, lesser_im = split(lesser)
    greater_re = lesser_re + full_re - swap(full_re)
    greater_im = lesser_im + full_im + swap(full_im)

    chunks = lax.axis_size("energy") * lax.axis_size("space")
    row_count = order // chunks
    parts = [lesser_re, lesser_im, greater_re, greater_im]
    parts = [part.reshape((energies_here, chunks, row_count, order)) for part in parts]
    paired = jnp.moveaxis(jnp.stack(parts, axis=2), 1, 0)
    arrived = lax.all_to_all(paired, ("energy", "space"), split_axis=0, concat_axis=0, tiled=True)
    arrived = arrived.reshape(
        (lax.axis_size("energy"), lax.axis_size("space"), energies_here, 4, row_count, order)
    )
    arrived = jnp.transpose(arrived, (0, 2, 1, 3, 4, 5))
    regrouped = arrived.reshape((total, lax.axis_size("space"), 2, 2, row_count, order))
    a_re, a_im = regrouped[:, :, 0, 0], regrouped[:, :, 0, 1]
    b_re, b_im = regrouped[:, :, 1, 0], regrouped[:, :, 1, 1]
    corr_re = []
    corr_im = []
    for shift_index in range(total):
        upper_re, upper_im = a_re[shift_index:], a_im[shift_index:]
        lower_re, lower_im = b_re[: total - shift_index], b_im[: total - shift_index]
        corr_re.append(jnp.sum(upper_re * lower_re + upper_im * lower_im, axis=0))
        corr_im.append(jnp.sum(upper_im * lower_re - upper_re * lower_im, axis=0))
    corr_re = jnp.stack(corr_re, axis=0)
    corr_im = jnp.stack(corr_im, axis=0)
    return jnp.stack([-order * corr_im, order * corr_re], axis=2)


def solution(mesh):
    return jax.shard_map(
        body,
        mesh=mesh,
        in_specs=(
            P("space", None, "groups", None),
            P("groups", None, None, None),
            P("energy", "space", "groups"),
            P("energy", "space", "groups"),
            P("energy", "space", "groups"),
        ),
        out_specs=P("groups", None, None, ("energy", "space"), None),
        check_vma=False,
    )
```

```python
import jax
import jax.numpy as jnp
from jax import lax
from jax.sharding import PartitionSpec as P


def from_partner(shard, axis, distance):
    return lax.ppermute(shard, axis, [(i, i ^ 1 << distance) for i in range(lax.axis_size(axis))])


def dot(left, right, precision=lax.Precision.HIGHEST):
    return jnp.einsum("...ij,...jk->...ik", left, right, precision=precision)


def swap(value):
    return jnp.swapaxes(value, -1, -2)


def embed(real, imag):
    top = jnp.concatenate([real, -imag], axis=-1)
    bottom = jnp.concatenate([imag, real], axis=-1)
    return jnp.concatenate([top, bottom], axis=-2)


def stack(real, imag):
    return jnp.concatenate([real, imag], axis=-2)


def split(stacked):
    order = stacked.shape[-2] // 2
    return stacked[..., :order, :], stacked[..., order:, :]


def stacked_adjoint(real, imag):
    return stack(swap(real), -swap(imag))


def invert(matrix):
    order = matrix.shape[-1] // 2
    eye = stack(jnp.eye(order, dtype=jnp.float32), jnp.zeros((order, order), jnp.float32))
    high = lax.Precision.HIGH
    gram = jnp.einsum("...ij,...kj->...ik", matrix, matrix[..., :order, :], precision=high)
    square = dot(embed(*split(gram)), gram, high)
    fourth = dot(embed(*split(square)), square, high)
    fourth_re, fourth_im = split(fourth)
    rows = jnp.sum(jnp.abs(fourth_re) + jnp.abs(fourth_im), axis=-1)
    beta = jnp.sqrt(jnp.sqrt(jnp.max(rows, axis=-1))) * 1.01 + 1e-30
    beta = beta[..., None, None]
    lower = 0.25 / beta
    alpha = 2.0 / (lower + 1.0)
    base = jnp.einsum("...ji,...jk->...ik", matrix, eye, precision=high)
    cubic = jnp.einsum("...ji,...jk->...ik", matrix, gram, precision=high)
    scale = alpha / beta
    approx = (2.0 * scale) * base - (scale * scale) * cubic
    ratio = (1.0 - lower) / (1.0 + lower)
    lower = 1.0 - ratio * ratio
    for _ in range(5):
        alpha = 2.0 / (lower + 1.0)
        product = dot(matrix, approx, high)
        approx = dot(alpha * embed(*split(approx)), 2.0 * eye - alpha * product, high)
        ratio = (1.0 - lower) / (1.0 + lower)
        lower = 1.0 - ratio * ratio

    def keep_going(state):
        _, residual, count = state
        return (residual > 2e-3) & (count < 40)

    def newton(state):
        approx, _, count = state
        rest = eye - dot(matrix, approx)
        residual = jnp.sqrt(jnp.max(jnp.sum(rest * rest, axis=(-1, -2))))
        return approx + dot(embed(*split(approx)), rest, high), residual, count + 1

    approx, _, _ = lax.while_loop(
        keep_going, newton, (approx, jnp.float32(jnp.inf), jnp.int32(0))
    )
    return approx


def body(ham_diag, ham_coupling, sigma_shift, sigma_width, occupation):
    blocks = ham_diag.shape[0]
    assert blocks == 1
    energies_here = sigma_shift.shape[0]
    order = ham_diag.shape[-1]
    side = lax.axis_index("space")
    first = side == 0
    total = energies_here * lax.axis_size("energy")
    offset = lax.axis_index("energy") * energies_here
    energy = -2.0 + 4.0 * ((offset + jnp.arange(energies_here)).astype(jnp.float32) + 0.5) / total
    identity = jnp.eye(order, dtype=jnp.float32)
    shift = sigma_shift[:, 0]
    width = sigma_width[:, 0]
    source = 2.0 * occupation[:, 0] * width
    real_part = (
        energy[:, None, None] * identity
        - ham_diag[None, 0, 0]
        - shift[:, :, None] * identity
    )
    imag_part = width[:, :, None] * identity - ham_diag[None, 0, 1]
    system = embed(real_part, imag_part)

    green_col = invert(system)
    g_re, g_im = split(green_col)
    scaled = embed(-g_im * source[:, None, :], g_re * source[:, None, :])
    link = ham_coupling[0]
    link_re = jnp.where(first, swap(link[0]), link[0])
    link_im = jnp.where(first, -swap(link[1]), link[1])
    link_embed = embed(link_re, link_im)
    link_adj = stacked_adjoint(link_re, link_im)
    high = lax.Precision.HIGH
    left_green = dot(link_embed, green_col, high)
    coupled_green = from_partner(dot(embed(*split(left_green)), link_adj, high), "space", 0)
    green_less = dot(scaled, stacked_adjoint(g_re, g_im), high)
    left_less = dot(link_embed, green_less, high)
    coupled_less = from_partner(dot(embed(*split(left_less)), link_adj, high), "space", 0)

    full_re, full_im = split(invert(system - embed(*split(coupled_green))))
    less_re, less_im = split(coupled_less)
    less_im = less_im + source[:, :, None] * identity
    inner = dot(embed(full_re, full_im), stack(less_re, less_im), high)
    lesser = dot(embed(*split(inner)), stacked_adjoint(full_re, full_im), high)
    lesser_re, lesser_im = split(lesser)
    greater_re = lesser_re + full_re - swap(full_re)
    greater_im = lesser_im + full_im + swap(full_im)

    chunks = lax.axis_size("energy") * lax.axis_size("space")
    row_count = order // chunks
    parts = [lesser_re, lesser_im, greater_re, greater_im]
    parts = [part.reshape((energies_here, chunks, row_count, order)) for part in parts]
    paired = jnp.moveaxis(jnp.stack(parts, axis=2), 1, 0)
    arrived = lax.all_to_all(paired, ("energy", "space"), split_axis=0, concat_axis=0, tiled=True)
    arrived = arrived.reshape(
        (lax.axis_size("energy"), lax.axis_size("space"), energies_here, 4, row_count, order)
    )
    arrived = jnp.transpose(arrived, (0, 2, 1, 3, 4, 5))
    regrouped = arrived.reshape((total, lax.axis_size("space"), 2, 2, row_count, order))
    a_re, a_im = regrouped[:, :, 0, 0], regrouped[:, :, 0, 1]
    b_re, b_im = regrouped[:, :, 1, 0], regrouped[:, :, 1, 1]
    corr_re = []
    corr_im = []
    for shift_index in range(total):
        upper_re, upper_im = a_re[shift_index:], a_im[shift_index:]
        lower_re, lower_im = b_re[: total - shift_index], b_im[: total - shift_index]
        corr_re.append(jnp.sum(upper_re * lower_re + upper_im * lower_im, axis=0))
        corr_im.append(jnp.sum(upper_im * lower_re - upper_re * lower_im, axis=0))
    corr_re = jnp.stack(corr_re, axis=0)
    corr_im = jnp.stack(corr_im, axis=0)
    return jnp.stack([-order * corr_im, order * corr_re], axis=2)


def solution(mesh):
    return jax.shard_map(
        body,
        mesh=mesh,
        in_specs=(
            P("space", None, "groups", None),
            P("groups", None, None, None),
            P("energy", "space", "groups"),
            P("energy", "space", "groups"),
            P("energy", "space", "groups"),
        ),
        out_specs=P("groups", None, None, ("energy", "space"), None),
        check_vma=False,
    )
```

```python
import jax
import jax.numpy as jnp
from jax import lax
from jax.sharding import PartitionSpec as P


def from_partner(shard, axis, distance):
    return lax.ppermute(shard, axis, [(i, i ^ 1 << distance) for i in range(lax.axis_size(axis))])


def dot(left, right, precision=lax.Precision.HIGHEST):
    return jnp.einsum("...ij,...jk->...ik", left, right, precision=precision)


def swap(value):
    return jnp.swapaxes(value, -1, -2)


def embed(real, imag):
    top = jnp.concatenate([real, -imag], axis=-1)
    bottom = jnp.concatenate([imag, real], axis=-1)
    return jnp.concatenate([top, bottom], axis=-2)


def stack(real, imag):
    return jnp.concatenate([real, imag], axis=-2)


def split(stacked):
    order = stacked.shape[-2] // 2
    return stacked[..., :order, :], stacked[..., order:, :]


def stacked_adjoint(real, imag):
    return stack(swap(real), -swap(imag))


def invert(matrix):
    order = matrix.shape[-1] // 2
    eye = stack(jnp.eye(order, dtype=jnp.float32), jnp.zeros((order, order), jnp.float32))
    high = lax.Precision.HIGH
    gram = jnp.einsum("...ij,...kj->...ik", matrix, matrix[..., :order, :], precision=high)
    square = dot(embed(*split(gram)), gram, high)
    fourth = dot(embed(*split(square)), square, high)
    fourth_re, fourth_im = split(fourth)
    rows = jnp.sum(jnp.abs(fourth_re) + jnp.abs(fourth_im), axis=-1)
    largest = jnp.max(rows, axis=-1, keepdims=True)[..., None, :]
    largest = jnp.broadcast_to(largest, largest.shape[:-1] + (2 * order,))
    beta = jnp.sqrt(jnp.sqrt(largest)) * 1.01 + 1e-30
    lower = 0.25 / beta
    alpha = 2.0 / (lower + 1.0)
    scale = (alpha / beta)[..., :order]
    first_step = 2.0 * eye - scale * gram
    approx = jnp.einsum("...ji,...jk->...ik", matrix, first_step, precision=high) * scale
    ratio = (1.0 - lower) / (1.0 + lower)
    lower = 1.0 - ratio * ratio
    for _ in range(5):
        alpha = 2.0 / (lower + 1.0)
        product = dot(matrix, approx, high)
        approx = dot(alpha * embed(*split(approx)), 2.0 * eye - alpha[..., :order] * product, high)
        ratio = (1.0 - lower) / (1.0 + lower)
        lower = 1.0 - ratio * ratio

    def keep_going(state):
        _, residual, count = state
        return (residual > 2e-3) & (count < 40)

    def newton(state):
        approx, _, count = state
        rest = eye - dot(matrix, approx)
        residual = jnp.sqrt(jnp.max(jnp.sum(rest * rest, axis=(-1, -2))))
        return approx + dot(embed(*split(approx)), rest, high), residual, count + 1

    approx, _, _ = lax.while_loop(
        keep_going, newton, (approx, jnp.float32(jnp.inf), jnp.int32(0))
    )
    return approx


def body(ham_diag, ham_coupling, sigma_shift, sigma_width, occupation):
    blocks = ham_diag.shape[0]
    assert blocks == 1
    energies_here = sigma_shift.shape[0]
    order = ham_diag.shape[-1]
    side = lax.axis_index("space")
    first = side == 0
    total = energies_here * lax.axis_size("energy")
    offset = lax.axis_index("energy") * energies_here
    energy = -2.0 + 4.0 * ((offset + jnp.arange(energies_here)).astype(jnp.float32) + 0.5) / total
    identity = jnp.eye(order, dtype=jnp.float32)
    shift = sigma_shift[:, 0]
    width = sigma_width[:, 0]
    source = 2.0 * occupation[:, 0] * width
    real_part = (
        energy[:, None, None] * identity
        - ham_diag[None, 0, 0]
        - shift[:, :, None] * identity
    )
    imag_part = width[:, :, None] * identity - ham_diag[None, 0, 1]
    system = embed(real_part, imag_part)

    green_col = invert(system)
    g_re, g_im = split(green_col)
    scaled = embed(-g_im * source[:, None, :], g_re * source[:, None, :])
    link = ham_coupling[0]
    link_re = jnp.where(first, swap(link[0]), link[0])
    link_im = jnp.where(first, -swap(link[1]), link[1])
    link_embed = embed(link_re, link_im)
    link_adj = stacked_adjoint(link_re, link_im)
    high = lax.Precision.HIGH
    left_green = dot(link_embed, green_col, high)
    coupled_green = from_partner(dot(embed(*split(left_green)), link_adj, high), "space", 0)
    green_less = dot(scaled, stacked_adjoint(g_re, g_im), high)
    left_less = dot(link_embed, green_less, high)
    coupled_less = from_partner(dot(embed(*split(left_less)), link_adj, high), "space", 0)

    full_re, full_im = split(invert(system - embed(*split(coupled_green))))
    less_re, less_im = split(coupled_less)
    less_im = less_im + source[:, :, None] * identity
    inner = dot(embed(full_re, full_im), stack(less_re, less_im), high)
    lesser = dot(embed(*split(inner)), stacked_adjoint(full_re, full_im), high)
    lesser_re, lesser_im = split(lesser)
    greater_re = lesser_re + full_re - swap(full_re)
    greater_im = lesser_im + full_im + swap(full_im)

    chunks = lax.axis_size("energy") * lax.axis_size("space")
    row_count = order // chunks
    parts = [lesser_re, lesser_im, greater_re, greater_im]
    parts = [part.reshape((energies_here, chunks, row_count, order)) for part in parts]
    paired = jnp.moveaxis(jnp.stack(parts, axis=2), 1, 0)
    arrived = lax.all_to_all(paired, ("energy", "space"), split_axis=0, concat_axis=0, tiled=True)
    arrived = arrived.reshape(
        (lax.axis_size("energy"), lax.axis_size("space"), energies_here, 4, row_count, order)
    )
    arrived = jnp.transpose(arrived, (0, 2, 1, 3, 4, 5))
    regrouped = arrived.reshape((total, lax.axis_size("space"), 2, 2, row_count, order))
    a_re, a_im = regrouped[:, :, 0, 0], regrouped[:, :, 0, 1]
    b_re, b_im = regrouped[:, :, 1, 0], regrouped[:, :, 1, 1]
    corr_re = []
    corr_im = []
    for shift_index in range(total):
        upper_re, upper_im = a_re[shift_index:], a_im[shift_index:]
        lower_re, lower_im = b_re[: total - shift_index], b_im[: total - shift_index]
        corr_re.append(jnp.sum(upper_re * lower_re + upper_im * lower_im, axis=0))
        corr_im.append(jnp.sum(upper_im * lower_re - upper_re * lower_im, axis=0))
    corr_re = jnp.stack(corr_re, axis=0)
    corr_im = jnp.stack(corr_im, axis=0)
    return jnp.stack([-order * corr_im, order * corr_re], axis=2)


def solution(mesh):
    return jax.shard_map(
        body,
        mesh=mesh,
        in_specs=(
            P("space", None, "groups", None),
            P("groups", None, None, None),
            P("energy", "space", "groups"),
            P("energy", "space", "groups"),
            P("energy", "space", "groups"),
        ),
        out_specs=P("groups", None, None, ("energy", "space"), None),
        check_vma=False,
    )
```

```python
import jax
import jax.numpy as jnp
from jax import lax
from jax.sharding import PartitionSpec as P


def from_partner(shard, axis, distance):
    return lax.ppermute(shard, axis, [(i, i ^ 1 << distance) for i in range(lax.axis_size(axis))])


def dot(left, right, precision=lax.Precision.HIGHEST):
    return jnp.einsum("...ij,...jk->...ik", left, right, precision=precision)


def swap(value):
    return jnp.swapaxes(value, -1, -2)


def embed(real, imag):
    top = jnp.concatenate([real, -imag], axis=-1)
    bottom = jnp.concatenate([imag, real], axis=-1)
    return jnp.concatenate([top, bottom], axis=-2)


def stack(real, imag):
    return jnp.concatenate([real, imag], axis=-2)


def split(stacked):
    order = stacked.shape[-2] // 2
    return stacked[..., :order, :], stacked[..., order:, :]


def stacked_adjoint(real, imag):
    return stack(swap(real), -swap(imag))


def invert(matrix):
    order = matrix.shape[-1] // 2
    eye = stack(jnp.eye(order, dtype=jnp.float32), jnp.zeros((order, order), jnp.float32))
    high = lax.Precision.HIGH
    gram = jnp.einsum("...ij,...kj->...ik", matrix, matrix[..., :order, :], precision=high)
    square = dot(embed(*split(gram)), gram, high)
    fourth = dot(embed(*split(square)), square, high)
    fourth_re, fourth_im = split(fourth)
    rows = jnp.sum(jnp.abs(fourth_re) + jnp.abs(fourth_im), axis=-1)
    beta = jnp.sqrt(jnp.sqrt(jnp.max(rows, axis=-1))) * 1.01 + 1e-30
    beta = beta[..., None, None]
    lower = 0.25 / beta
    alpha = 2.0 / (lower + 1.0)
    first_step = 2.0 * eye - (alpha / beta) * gram
    approx = jnp.einsum("...ji,...jk->...ik", matrix, first_step, precision=high) * (alpha / beta)
    ratio = (1.0 - lower) / (1.0 + lower)
    lower = 1.0 - ratio * ratio
    for _ in range(5):
        alpha = 2.0 / (lower + 1.0)
        product = dot(matrix, approx, high)
        approx = dot(alpha * embed(*split(approx)), 2.0 * eye - alpha * product, high)
        ratio = (1.0 - lower) / (1.0 + lower)
        lower = 1.0 - ratio * ratio

    def keep_going(state):
        _, residual, count = state
        return (residual > 4e-6) & (count < 40)

    def newton(state):
        approx, _, count = state
        rest = eye - dot(matrix, approx)
        residual = jnp.max(jnp.sum(rest * rest, axis=(-1, -2)))
        return approx + dot(embed(*split(approx)), rest, high), residual, count + 1

    approx, _, _ = lax.while_loop(
        keep_going, newton, (approx, jnp.float32(jnp.inf), jnp.int32(0))
    )
    return approx


def body(ham_diag, ham_coupling, sigma_shift, sigma_width, occupation):
    blocks = ham_diag.shape[0]
    assert blocks == 1
    energies_here = sigma_shift.shape[0]
    order = ham_diag.shape[-1]
    side = lax.axis_index("space")
    first = side == 0
    total = energies_here * lax.axis_size("energy")
    offset = lax.axis_index("energy") * energies_here
    energy = -2.0 + 4.0 * ((offset + jnp.arange(energies_here)).astype(jnp.float32) + 0.5) / total
    identity = jnp.eye(order, dtype=jnp.float32)
    shift = sigma_shift[:, 0]
    width = sigma_width[:, 0]
    source = 2.0 * occupation[:, 0] * width
    real_part = (
        energy[:, None, None] * identity
        - ham_diag[None, 0, 0]
        - shift[:, :, None] * identity
    )
    imag_part = width[:, :, None] * identity - ham_diag[None, 0, 1]
    system = embed(real_part, imag_part)

    green_col = invert(system)
    g_re, g_im = split(green_col)
    scaled = embed(-g_im * source[:, None, :], g_re * source[:, None, :])
    link = ham_coupling[0]
    link_re = jnp.where(first, swap(link[0]), link[0])
    link_im = jnp.where(first, -swap(link[1]), link[1])
    link_embed = embed(link_re, link_im)
    link_adj = stacked_adjoint(link_re, link_im)
    high = lax.Precision.HIGH
    left_green = dot(link_embed, green_col, high)
    coupled_green = from_partner(dot(embed(*split(left_green)), link_adj, high), "space", 0)
    green_less = dot(scaled, stacked_adjoint(g_re, g_im), high)
    left_less = dot(link_embed, green_less, high)
    coupled_less = from_partner(dot(embed(*split(left_less)), link_adj, high), "space", 0)

    full_re, full_im = split(invert(system - embed(*split(coupled_green))))
    less_re, less_im = split(coupled_less)
    less_im = less_im + source[:, :, None] * identity
    inner = dot(embed(full_re, full_im), stack(less_re, less_im), high)
    lesser = dot(embed(*split(inner)), stacked_adjoint(full_re, full_im), high)
    lesser_re, lesser_im = split(lesser)
    greater_re = lesser_re + full_re - swap(full_re)
    greater_im = lesser_im + full_im + swap(full_im)

    chunks = lax.axis_size("energy") * lax.axis_size("space")
    row_count = order // chunks
    parts = [lesser_re, lesser_im, greater_re, greater_im]
    parts = [part.reshape((energies_here, chunks, row_count, order)) for part in parts]
    paired = jnp.moveaxis(jnp.stack(parts, axis=2), 1, 0)
    arrived = lax.all_to_all(paired, ("energy", "space"), split_axis=0, concat_axis=0, tiled=True)
    arrived = arrived.reshape(
        (lax.axis_size("energy"), lax.axis_size("space"), energies_here, 4, row_count, order)
    )
    arrived = jnp.transpose(arrived, (0, 2, 1, 3, 4, 5))
    regrouped = arrived.reshape((total, lax.axis_size("space"), 2, 2, row_count, order))
    a_re, a_im = regrouped[:, :, 0, 0], regrouped[:, :, 0, 1]
    b_re, b_im = regrouped[:, :, 1, 0], regrouped[:, :, 1, 1]
    corr_re = []
    corr_im = []
    for shift_index in range(total):
        upper_re, upper_im = a_re[shift_index:], a_im[shift_index:]
        lower_re, lower_im = b_re[: total - shift_index], b_im[: total - shift_index]
        corr_re.append(jnp.sum(upper_re * lower_re + upper_im * lower_im, axis=0))
        corr_im.append(jnp.sum(upper_im * lower_re - upper_re * lower_im, axis=0))
    corr_re = jnp.stack(corr_re, axis=0)
    corr_im = jnp.stack(corr_im, axis=0)
    return jnp.stack([-order * corr_im, order * corr_re], axis=2)


def solution(mesh):
    return jax.shard_map(
        body,
        mesh=mesh,
        in_specs=(
            P("space", None, "groups", None),
            P("groups", None, None, None),
            P("energy", "space", "groups"),
            P("energy", "space", "groups"),
            P("energy", "space", "groups"),
        ),
        out_specs=P("groups", None, None, ("energy", "space"), None),
        check_vma=False,
    )
```

```python
import jax
import jax.numpy as jnp
from jax import lax
from jax.sharding import PartitionSpec as P


def from_partner(shard, axis, distance):
    return lax.ppermute(shard, axis, [(i, i ^ 1 << distance) for i in range(lax.axis_size(axis))])


def dot(left, right, precision=lax.Precision.HIGHEST):
    return jnp.einsum("...ij,...jk->...ik", left, right, precision=precision)


def swap(value):
    return jnp.swapaxes(value, -1, -2)


def embed(real, imag):
    top = jnp.concatenate([real, -imag], axis=-1)
    bottom = jnp.concatenate([imag, real], axis=-1)
    return jnp.concatenate([top, bottom], axis=-2)


def stack(real, imag):
    return jnp.concatenate([real, imag], axis=-2)


def split(stacked):
    order = stacked.shape[-2] // 2
    return stacked[..., :order, :], stacked[..., order:, :]


def stacked_adjoint(real, imag):
    return stack(swap(real), -swap(imag))


def invert(matrix):
    order = matrix.shape[-1] // 2
    eye = stack(jnp.eye(order, dtype=jnp.float32), jnp.zeros((order, order), jnp.float32))
    high = lax.Precision.HIGH
    gram = jnp.einsum("...ij,...kj->...ik", matrix, matrix[..., :order, :], precision=high)
    square = dot(embed(*split(gram)), gram, high)
    fourth = dot(embed(*split(square)), square, high)
    fourth_re, fourth_im = split(fourth)
    rows = jnp.sum(jnp.abs(fourth_re) + jnp.abs(fourth_im), axis=-1)
    beta = jnp.sqrt(jnp.sqrt(jnp.max(rows, axis=-1) * 1.0406))
    beta = beta[..., None, None]
    lower = 0.25 / beta
    alpha = 2.0 / (lower + 1.0)
    first_step = 2.0 * eye - (alpha / beta) * gram
    approx = jnp.einsum("...ji,...jk->...ik", matrix, first_step, precision=high) * (alpha / beta)
    ratio = (1.0 - lower) / (1.0 + lower)
    lower = 1.0 - ratio * ratio
    for _ in range(5):
        alpha = 2.0 / (lower + 1.0)
        product = dot(matrix, approx, high)
        approx = dot(alpha * embed(*split(approx)), 2.0 * eye - alpha * product, high)
        ratio = (1.0 - lower) / (1.0 + lower)
        lower = 1.0 - ratio * ratio

    def keep_going(state):
        _, residual, count = state
        return (residual > 4e-6) & (count < 40)

    def newton(state):
        approx, _, count = state
        rest = eye - dot(matrix, approx)
        residual = jnp.max(jnp.sum(rest * rest, axis=(-1, -2)))
        return approx + dot(embed(*split(approx)), rest, high), residual, count + 1

    approx, _, _ = lax.while_loop(
        keep_going, newton, (approx, jnp.float32(jnp.inf), jnp.int32(0))
    )
    return approx


def body(ham_diag, ham_coupling, sigma_shift, sigma_width, occupation):
    blocks = ham_diag.shape[0]
    assert blocks == 1
    energies_here = sigma_shift.shape[0]
    order = ham_diag.shape[-1]
    side = lax.axis_index("space")
    first = side == 0
    total = energies_here * lax.axis_size("energy")
    offset = lax.axis_index("energy") * energies_here
    energy = -2.0 + 4.0 * ((offset + jnp.arange(energies_here)).astype(jnp.float32) + 0.5) / total
    identity = jnp.eye(order, dtype=jnp.float32)
    shift = sigma_shift[:, 0]
    width = sigma_width[:, 0]
    source = 2.0 * occupation[:, 0] * width
    real_part = (
        energy[:, None, None] * identity
        - ham_diag[None, 0, 0]
        - shift[:, :, None] * identity
    )
    imag_part = width[:, :, None] * identity - ham_diag[None, 0, 1]
    system = embed(real_part, imag_part)

    green_col = invert(system)
    g_re, g_im = split(green_col)
    scaled = embed(-g_im * source[:, None, :], g_re * source[:, None, :])
    link = ham_coupling[0]
    link_re = jnp.where(first, swap(link[0]), link[0])
    link_im = jnp.where(first, -swap(link[1]), link[1])
    link_embed = embed(link_re, link_im)
    link_adj = stacked_adjoint(link_re, link_im)
    high = lax.Precision.HIGH
    left_green = dot(link_embed, green_col, high)
    coupled_green = from_partner(dot(embed(*split(left_green)), link_adj, high), "space", 0)
    green_less = dot(scaled, stacked_adjoint(g_re, g_im), high)
    left_less = dot(link_embed, green_less, high)
    coupled_less = from_partner(dot(embed(*split(left_less)), link_adj, high), "space", 0)

    full_re, full_im = split(invert(system - embed(*split(coupled_green))))
    less_re, less_im = split(coupled_less)
    less_im = less_im + source[:, :, None] * identity
    inner = dot(embed(full_re, full_im), stack(less_re, less_im), high)
    lesser = dot(embed(*split(inner)), stacked_adjoint(full_re, full_im), high)
    lesser_re, lesser_im = split(lesser)
    greater_re = lesser_re + full_re - swap(full_re)
    greater_im = lesser_im + full_im + swap(full_im)

    chunks = lax.axis_size("energy") * lax.axis_size("space")
    row_count = order // chunks
    parts = [lesser_re, lesser_im, greater_re, greater_im]
    parts = [part.reshape((energies_here, chunks, row_count, order)) for part in parts]
    paired = jnp.moveaxis(jnp.stack(parts, axis=2), 1, 0)
    arrived = lax.all_to_all(paired, ("energy", "space"), split_axis=0, concat_axis=0, tiled=True)
    arrived = arrived.reshape(
        (lax.axis_size("energy"), lax.axis_size("space"), energies_here, 4, row_count, order)
    )
    arrived = jnp.transpose(arrived, (0, 2, 1, 3, 4, 5))
    regrouped = arrived.reshape((total, lax.axis_size("space"), 2, 2, row_count, order))
    a_re, a_im = regrouped[:, :, 0, 0], regrouped[:, :, 0, 1]
    b_re, b_im = regrouped[:, :, 1, 0], regrouped[:, :, 1, 1]
    corr_re = []
    corr_im = []
    for shift_index in range(total):
        upper_re, upper_im = a_re[shift_index:], a_im[shift_index:]
        lower_re, lower_im = b_re[: total - shift_index], b_im[: total - shift_index]
        corr_re.append(jnp.sum(upper_re * lower_re + upper_im * lower_im, axis=0))
        corr_im.append(jnp.sum(upper_im * lower_re - upper_re * lower_im, axis=0))
    corr_re = jnp.stack(corr_re, axis=0)
    corr_im = jnp.stack(corr_im, axis=0)
    return jnp.stack([-order * corr_im, order * corr_re], axis=2)


def solution(mesh):
    return jax.shard_map(
        body,
        mesh=mesh,
        in_specs=(
            P("space", None, "groups", None),
            P("groups", None, None, None),
            P("energy", "space", "groups"),
            P("energy", "space", "groups"),
            P("energy", "space", "groups"),
        ),
        out_specs=P("groups", None, None, ("energy", "space"), None),
        check_vma=False,
    )
```
